32 devices in a mesh: seq: 4 (over y, x), dp: 8 (over z, core).
Axes of the slice: x: 2, y: 2, z: 4, core: 2. Of those that a mesh axis runs over, the one named last changes fastest.
Arguments:
- queries: bfloat16 [8, 512, 4096], P('dp', 'seq'), may hold values from -6 to 6
- keys: bfloat16 [8, 512, 4096], P('dp', 'seq'), may hold values from -6 to 6
- values: bfloat16 [8, 512, 4096], P('dp', 'seq'), may hold values from -6 to 6
- cotangent: bfloat16 [8, 512, 4096], P('dp', 'seq'), may hold values from -6 to 6
- taps: float32 [3, 7, 4096], replicated, may hold values from -2 to 2
- residue: float32 [16, 4096], replicated, may hold values from -0.12 to 0.12
- skip: float32 [4096], replicated, may hold values from 0.5 to 1.5
- decay: float32 [16, 4096], replicated, may hold values from 0.0001953125 to 0.06
Outputs:
- mixed: bfloat16 [8, 512, 4096], P('dp', 'seq')
- grad_queries: bfloat16 [8, 512, 4096], P('dp', 'seq')
- grad_keys: bfloat16 [8, 512, 4096], P('dp', 'seq')
- grad_values: bfloat16 [8, 512, 4096], P('dp', 'seq')
- grad_taps: float32 [3, 7, 4096], replicated
- grad_residue: float32 [16, 4096], replicated
- grad_skip: float32 [4096], replicated
The draws below stay inside these ranges and needn't reach their ends.
All inputs are finite; a program needn't handle non-finite values.
Results may differ from the reference program's by a relative error of at most 0.001.
Values may be sent and summed in bfloat16 or wider, within the bound.
No kernel may reach another device: no remote copies, remote signals or barrier semaphores. Data moves between devices by JAX's collectives and lax.ppermute only.
A program may use at most 256 MiB of HBM per device.

```python
import math
import jax
import jax.numpy as jnp
from jax import lax

D = 4096
POLES = 16
TAPS = 7
BLOCK = 16
LENGTH = 512
BATCH = 8


def shard_levels(stream_key, extent, shards, least, largest):
    def one(dim, blocks):
        draws = jax.random.uniform(jax.random.fold_in(jax.random.fold_in(stream_key, 6), dim), (blocks,), jnp.float32, least / len(shards), largest / len(shards))
        return jnp.repeat(jnp.exp(draws), extent[dim] // blocks).reshape((-1,) + (1,) * (len(extent) - dim - 1))

    gain = one(*shards[0])
    for cut in shards[1:]:
        gain = gain * one(*cut)
    return gain


def gaussian(own_key, dims, deviation, bound, split=(), kind=jnp.bfloat16):
    values = jax.random.normal(own_key, dims, jnp.float32) * deviation
    if len(split) > 0:
        values = shard_levels(own_key, dims, split, -0.22, 0.18) * values
    return jnp.clip(values, min=-bound, max=bound).astype(kind)


def setup_inputs(seed: int = 0) -> dict:
    key_of = jax.random.split(jax.random.key(seed), 9)
    queries = gaussian(key_of[0], (BATCH, LENGTH, D), 1.0, 6.0, ((0, 8), (1, 4)))
    keys = gaussian(key_of[1], (BATCH, LENGTH, D), 1.0, 6.0, ((0, 8), (1, 4)))
    values = gaussian(key_of[2], (BATCH, LENGTH, D), 1.0, 6.0, ((0, 8), (1, 4)))
    cotangent = gaussian(key_of[3], (BATCH, LENGTH, D), 1.0, 6.0, ((0, 8), (1, 4)))
    taps = gaussian(key_of[4], (3, TAPS, D), TAPS ** -0.5, 2.0, (), jnp.float32)
    residue = gaussian(key_of[5], (POLES, D), 0.02, 0.12, (), jnp.float32)
    skip = jnp.clip(jax.random.uniform(key_of[6], (D,), jnp.float32, 0.5, 1.5), 0.5, 1.5)
    decay = jnp.clip(jnp.exp(jax.random.uniform(key_of[7], (POLES, D), jnp.float32, math.log(0.0001953125), math.log(0.06))), 0.0001953125, 0.06)
    return {"queries": queries, "keys": keys, "values": values, "cotangent": cotangent, "taps": taps, "residue": residue, "skip": skip, "decay": decay}


highest = lax.Precision.HIGHEST

def make_tables(decay, residue, width):
    steps = jnp.arange(width).astype(decay.dtype)
    power = jnp.exp(-decay[None] * steps[:, None, None])
    lag_filter = jnp.einsum('jnc,nc->jc', power, residue, precision=highest)
    ahead = jnp.arange(width)[:, None] - jnp.arange(width)[None, :]
    onehot = (ahead[:, :, None] == jnp.arange(width)[None, None, :]).astype(decay.dtype)
    toeplitz = jnp.einsum('isj,jc->isc', onehot, lag_filter, precision=highest)
    tail = power[::-1]
    decayed = power * jnp.exp(-decay)[None]
    head = decayed * residue[None]
    jump = jnp.exp(-decay * width)
    return (power, onehot, toeplitz, tail, decayed, head, jump)

def block_ends(stacked, tail):
    return jnp.einsum('bic,inc->bnc', stacked, tail, precision=highest)

def chain(ends, start, jump):

    def advance(state, end):
        return (jump * state + end, state)
    final, starts = lax.scan(advance, start, ends)
    return (starts, final)

def convolve(stacked, starts, toeplitz, head):
    inner = jnp.einsum('bsc,isc->bic', stacked, toeplitz, precision=highest)
    return inner + jnp.einsum('bnc,inc->bic', starts, head, precision=highest)

def featurize(padded, weights):
    margin = weights.shape[0] - 1
    count = padded.shape[0] - margin
    total = jnp.zeros_like(padded[:count])
    for lag in range(weights.shape[0]):
        total = total + weights[lag] * padded[margin - lag:margin - lag + count]
    return total

def mixer(queries, keys, values, taps, residue, skip, decay):
    length, width = queries.shape
    margin = taps.shape[1] - 1
    front = jnp.zeros((margin, width), queries.dtype)
    feat_q = featurize(jnp.concatenate([front, queries], 0).astype(jnp.float32), taps[0])
    feat_k = featurize(jnp.concatenate([front, keys], 0).astype(jnp.float32), taps[1])
    feat_v = featurize(jnp.concatenate([front, values], 0).astype(jnp.float32), taps[2])
    product = feat_k * feat_v
    power, onehot, toeplitz, tail, decayed, head, jump = make_tables(decay, residue, BLOCK)
    stacked = product.reshape(length // BLOCK, BLOCK, width)
    ends = block_ends(stacked, tail)
    starts, final = chain(ends, jnp.zeros_like(jump), jump)
    conv = convolve(stacked, starts, toeplitz, head).reshape(length, width)
    return feat_q * (conv + skip * product)

def reference(queries, keys, values, cotangent, taps, residue, skip, decay):

    def one(carry, item):
        query, key, value, grad = item
        out, pull = jax.vjp(lambda a, b, c, w, r, s: mixer(a, b, c, w, r, s, decay), query, key, value, taps, residue, skip)
        grad_q, grad_k, grad_v, grad_w, grad_r, grad_s = pull(grad.astype(jnp.float32))
        carry = (carry[0] + grad_w, carry[1] + grad_r, carry[2] + grad_s)
        return (carry, (out.astype(jnp.bfloat16), grad_q, grad_k, grad_v))
    start = (jnp.zeros_like(taps), jnp.zeros_like(residue), jnp.zeros_like(skip))
    totals, outputs = lax.scan(one, start, (queries, keys, values, cotangent))
    return (outputs[0], outputs[1], outputs[2], outputs[3], totals[0], totals[1], totals[2])
```

```python
import functools

import jax
import jax.numpy as jnp
from jax import lax
from jax.experimental import pallas as pl
from jax.experimental.pallas import tpu as pltpu
from jax.sharding import PartitionSpec as P

LANES = 512
RIM = 8
TAIL = 16
F32 = jnp.float32


def passed_along(x, axis, by):
    count = lax.axis_size(axis)
    pairs = [(i, i + by) for i in range(count) if 0 <= i + by < count]
    return lax.ppermute(x, axis, pairs)


def load_padded(x_ref, rim_ref, pad_ref, s):
    rows = x_ref.shape[0]
    pad_ref[s, 0:RIM, :] = rim_ref[s].astype(F32)
    pad_ref[s, RIM : RIM + rows, :] = x_ref[...].astype(F32)


def featurize(pad_ref, taps_ref, s, rows):
    count = taps_ref.shape[1]
    total = taps_ref[s, 0:1, :] * pad_ref[s, RIM : RIM + rows, :]
    for lag in range(1, count):
        total = total + taps_ref[s, lag : lag + 1, :] * pad_ref[s, RIM - lag : RIM - lag + rows, :]
    return total


def states_kernel(q_ref, k_ref, v_ref, c_ref, rim_ref, taps_ref, a_ref, f_ref, b_ref, pad_ref, p_ref, z_ref):
    rows = q_ref.shape[0]
    for s, x_ref in enumerate((q_ref, k_ref, v_ref)):
        load_padded(x_ref, rim_ref, pad_ref, s)
    fq = featurize(pad_ref, taps_ref, 0, rows)
    fk = featurize(pad_ref, taps_ref, 1, rows)
    fv = featurize(pad_ref, taps_ref, 2, rows)
    p_ref[...] = fk * fv
    z_ref[...] = c_ref[...].astype(F32) * fq
    a = a_ref[...]

    def step(i, carry):
        h, g = carry
        h = a * h + p_ref[pl.ds(i, 1), :]
        g = a * g + z_ref[pl.ds(rows - 1 - i, 1), :]
        return (h, g)

    zero = jnp.zeros_like(a)
    h, g = lax.fori_loop(0, rows, step, (zero, zero), unroll=8)
    f_ref[...] = h
    b_ref[...] = g


def main_kernel(
    q_ref, k_ref, v_ref, c_ref, rim_ref, taps_ref, a_ref, r_ref, skip_ref, s_ref, g_ref,
    mixed_ref, gq_ref, gk_ref, gv_ref, tail_ref, head_ref, grads_ref,
    pad_ref, p_ref, z_ref, y_ref, u_ref, adj_ref,
):
    rows = q_ref.shape[0]
    count = taps_ref.shape[1]
    poles = a_ref.shape[0]
    for s, x_ref in enumerate((q_ref, k_ref, v_ref)):
        load_padded(x_ref, rim_ref, pad_ref, s)
    fq = featurize(pad_ref, taps_ref, 0, rows)
    fk = featurize(pad_ref, taps_ref, 1, rows)
    fv = featurize(pad_ref, taps_ref, 2, rows)
    cot = c_ref[...].astype(F32)
    p_ref[...] = fk * fv
    z_ref[...] = cot * fq
    a = a_ref[...]
    r = r_ref[...]

    def step(i, carry):
        h, g, acc = carry
        h = a * h + p_ref[pl.ds(i, 1), :]
        acc = acc + z_ref[pl.ds(i, 1), :] * h
        y_ref[pl.ds(i, 1), :] = jnp.sum(r * h, axis=0, keepdims=True)
        back = rows - 1 - i
        g = a * g + z_ref[pl.ds(back, 1), :]
        u_ref[pl.ds(back, 1), :] = jnp.sum(r * g, axis=0, keepdims=True)
        return (h, g, acc)

    h, g, acc = lax.fori_loop(
        0, rows, step, (s_ref[...], g_ref[...], jnp.zeros_like(a)), unroll=8
    )
    skip = skip_ref[...]
    p = p_ref[...]
    z = z_ref[...]
    conv = y_ref[...] + skip * p
    mixed_ref[...] = (fq * conv).astype(mixed_ref.dtype)
    adj_u = u_ref[...] + skip * z
    adjoints = (cot * conv, adj_u * fv, adj_u * fk)
    zeros_rim = jnp.zeros((RIM, adj_ref.shape[2]), F32)
    outs = (gq_ref, gk_ref, gv_ref)
    for s in range(3):
        adj_ref[s, 0:rows, :] = adjoints[s]
        adj_ref[s, rows : rows + RIM, :] = zeros_rim
        head_ref[s] = adjoints[s][0:RIM]
        total = taps_ref[s, 0:1, :] * adjoints[s]
        for lag in range(1, count):
            total = total + taps_ref[s, lag : lag + 1, :] * adj_ref[s, lag : lag + rows, :]
        outs[s][...] = total.astype(outs[s].dtype)
        tail_ref[s] = total[rows - TAIL : rows]
        for lag in range(count):
            window = pad_ref[s, RIM - lag : RIM - lag + rows, :]
            row = s * count + lag
            grads_ref[row : row + 1, :] = jnp.sum(adjoints[s] * window, axis=0, keepdims=True)
    base = 3 * count
    grads_ref[base : base + poles, :] = acc
    grads_ref[base + poles : base + poles + 1, :] = jnp.sum(z * p, axis=0, keepdims=True)


def tile(shape, lanes):
    nd = len(shape)
    return pl.BlockSpec(tuple(shape[:-1]) + (lanes,), lambda i: (0,) * (nd - 1) + (i,))


def run_states(q, k, v, c, rim, taps, a):
    rows, width = q.shape
    poles = a.shape[0]
    lanes = min(LANES, width)
    ins = (q, k, v, c, rim, taps, a)
    return pl.pallas_call(
        states_kernel,
        grid=(width // lanes,),
        in_specs=[tile(x.shape, lanes) for x in ins],
        out_specs=[tile((poles, width), lanes), tile((poles, width), lanes)],
        out_shape=[jax.ShapeDtypeStruct((poles, width), F32)] * 2,
        scratch_shapes=[
            pltpu.VMEM((3, rows + RIM, lanes), F32),
            pltpu.VMEM((rows, lanes), F32),
            pltpu.VMEM((rows, lanes), F32),
        ],
    )(*ins)


def run_main(q, k, v, c, rim, taps, a, r, skip, s_in, g_in):
    rows, width = q.shape
    poles = a.shape[0]
    count = taps.shape[1]
    lanes = min(LANES, width)
    ins = (q, k, v, c, rim, taps, a, r, skip, s_in, g_in)
    out_shapes = [
        jax.ShapeDtypeStruct((rows, width), jnp.bfloat16),
        jax.ShapeDtypeStruct((rows, width), jnp.bfloat16),
        jax.ShapeDtypeStruct((rows, width), jnp.bfloat16),
        jax.ShapeDtypeStruct((rows, width), jnp.bfloat16),
        jax.ShapeDtypeStruct((3, TAIL, width), F32),
        jax.ShapeDtypeStruct((3, RIM, width), F32),
        jax.ShapeDtypeStruct((3 * count + poles + 1, width), F32),
    ]
    return pl.pallas_call(
        main_kernel,
        grid=(width // lanes,),
        in_specs=[tile(x.shape, lanes) for x in ins],
        out_specs=[tile(o.shape, lanes) for o in out_shapes],
        out_shape=out_shapes,
        scratch_shapes=[
            pltpu.VMEM((3, rows + RIM, lanes), F32),
            pltpu.VMEM((rows, lanes), F32),
            pltpu.VMEM((rows, lanes), F32),
            pltpu.VMEM((rows, lanes), F32),
            pltpu.VMEM((rows, lanes), F32),
            pltpu.VMEM((3, rows + RIM, lanes), F32),
        ],
    )(*ins)


def carried(final, decay, rows, axis, by):
    count = lax.axis_size(axis)
    window = final
    incoming = jnp.zeros_like(final)
    span = 1
    covered = 0
    while span < count:
        got = passed_along(window, axis, by * span)
        incoming = incoming + jnp.exp(-decay * (rows * covered)) * got
        window = window + jnp.exp(-decay * (rows * span)) * got
        covered += span
        span *= 2
    return incoming


def per_device(queries, keys, values, cotangent, taps, residue, skip, decay):
    rows = queries.shape[1]
    width = queries.shape[2]
    count = taps.shape[1]
    poles = decay.shape[0]
    q, k, v, c = queries[0], keys[0], values[0], cotangent[0]
    rim = passed_along(jnp.stack([q[rows - RIM :], k[rows - RIM :], v[rows - RIM :]], 0), "seq", 1)
    a = jnp.exp(-decay)
    f_local, b_local = run_states(q, k, v, c, rim, taps, a)
    with jax.named_scope("modal_state_scan"):
        s_in = carried(f_local, decay, rows, "seq", 1)
        g_in = carried(b_local, decay, rows, "seq", -1)
    mixed, gq, gk, gv, tails, heads, grads = run_main(
        q, k, v, c, rim, taps, a, residue, skip.reshape(1, width), s_in, g_in
    )
    after = passed_along(heads, "seq", -1)
    ext = jnp.concatenate(
        [jnp.zeros((3, TAIL, width), F32), after[:, : count - 1], jnp.zeros((3, 1, width), F32)], 1
    )
    corr = sum(taps[:, lag, None, :] * ext[:, lag : lag + TAIL] for lag in range(count))
    fixed = (tails + corr).astype(jnp.bfloat16)
    streams = [
        lax.dynamic_update_slice(g, fixed[idx], (rows - TAIL, 0)) for idx, g in enumerate((gq, gk, gv))
    ]
    totals = lax.psum(grads, ("seq", "dp"))
    grad_taps = totals[: 3 * count].reshape(3, count, width)
    grad_residue = totals[3 * count : 3 * count + poles]
    grad_skip = totals[3 * count + poles]
    return (
        mixed[None],
        streams[0][None],
        streams[1][None],
        streams[2][None],
        grad_taps,
        grad_residue,
        grad_skip,
    )


def solution(mesh):
    return jax.shard_map(
        per_device,
        mesh=mesh,
        in_specs=(
            P("dp", "seq", None),
            P("dp", "seq", None),
            P("dp", "seq", None),
            P("dp", "seq", None),
            P(),
            P(),
            P(),
            P(),
        ),
        out_specs=(
            P("dp", "seq", None),
            P("dp", "seq", None),
            P("dp", "seq", None),
            P("dp", "seq", None),
            P(),
            P(),
            P(),
        ),
        check_vma=False,
    )
```

```python
import functools

import jax
import jax.numpy as jnp
from jax import lax
from jax.experimental import pallas as pl
from jax.experimental.pallas import tpu as pltpu
from jax.sharding import PartitionSpec as P

LANES = 512
RIM = 8
TAIL = 16
F32 = jnp.float32


def passed_along(x, axis, by):
    count = lax.axis_size(axis)
    pairs = [(i, i + by) for i in range(count) if 0 <= i + by < count]
    return lax.ppermute(x, axis, pairs)


def load_padded(x_ref, rim_ref, pad_ref, s):
    rows = x_ref.shape[0]
    pad_ref[s, 0:RIM, :] = rim_ref[s].astype(F32)
    pad_ref[s, RIM : RIM + rows, :] = x_ref[...].astype(F32)


def featurize(pad_ref, taps_ref, s, rows):
    count = taps_ref.shape[1]
    total = taps_ref[s, 0:1, :] * pad_ref[s, RIM : RIM + rows, :]
    for lag in range(1, count):
        total = total + taps_ref[s, lag : lag + 1, :] * pad_ref[s, RIM - lag : RIM - lag + rows, :]
    return total


def states_kernel(q_ref, k_ref, v_ref, c_ref, rim_ref, taps_ref, a_ref, f_ref, b_ref, pad_ref, p_ref, z_ref):
    rows = q_ref.shape[0]
    for s, x_ref in enumerate((q_ref, k_ref, v_ref)):
        load_padded(x_ref, rim_ref, pad_ref, s)
    fq = featurize(pad_ref, taps_ref, 0, rows)
    fk = featurize(pad_ref, taps_ref, 1, rows)
    fv = featurize(pad_ref, taps_ref, 2, rows)
    p_ref[...] = fk * fv
    z_ref[...] = c_ref[...].astype(F32) * fq
    a = a_ref[...]

    def step(i, carry):
        h, g = carry
        h = a * h + p_ref[pl.ds(i, 1), :]
        g = a * g + z_ref[pl.ds(rows - 1 - i, 1), :]
        return (h, g)

    zero = jnp.zeros_like(a)
    h, g = lax.fori_loop(0, rows, step, (zero, zero), unroll=8)
    f_ref[...] = h
    b_ref[...] = g


def main_kernel(
    q_ref, k_ref, v_ref, c_ref, rim_ref, taps_ref, a_ref, r_ref, skip_ref, s_ref, g_ref,
    mixed_ref, gq_ref, gk_ref, gv_ref, tail_ref, head_ref, grads_ref,
    pad_ref, p_ref, z_ref, y_ref, u_ref, adj_ref,
):
    rows = q_ref.shape[0]
    count = taps_ref.shape[1]
    poles = a_ref.shape[0]
    for s, x_ref in enumerate((q_ref, k_ref, v_ref)):
        load_padded(x_ref, rim_ref, pad_ref, s)
    fq = featurize(pad_ref, taps_ref, 0, rows)
    fk = featurize(pad_ref, taps_ref, 1, rows)
    fv = featurize(pad_ref, taps_ref, 2, rows)
    cot = c_ref[...].astype(F32)
    p_ref[...] = fk * fv
    z_ref[...] = cot * fq
    a = a_ref[...]
    r = r_ref[...]

    def step(i, carry):
        h, g, acc = carry
        h = a * h + p_ref[pl.ds(i, 1), :]
        acc = acc + z_ref[pl.ds(i, 1), :] * h
        y_ref[pl.ds(i, 1), :] = jnp.sum(r * h, axis=0, keepdims=True)
        back = rows - 1 - i
        g = a * g + z_ref[pl.ds(back, 1), :]
        u_ref[pl.ds(back, 1), :] = jnp.sum(r * g, axis=0, keepdims=True)
        return (h, g, acc)

    h, g, acc = lax.fori_loop(
        0, rows, step, (s_ref[...], g_ref[...], jnp.zeros_like(a)), unroll=8
    )
    skip = skip_ref[...]
    p = p_ref[...]
    z = z_ref[...]
    conv = y_ref[...] + skip * p
    mixed_ref[...] = (fq * conv).astype(mixed_ref.dtype)
    adj_u = u_ref[...] + skip * z
    adjoints = (cot * conv, adj_u * fv, adj_u * fk)
    zeros_rim = jnp.zeros((RIM, adj_ref.shape[2]), F32)
    outs = (gq_ref, gk_ref, gv_ref)
    for s in range(3):
        adj_ref[s, 0:rows, :] = adjoints[s]
        adj_ref[s, rows : rows + RIM, :] = zeros_rim
        head_ref[s] = adjoints[s][0:RIM]
        total = taps_ref[s, 0:1, :] * adjoints[s]
        for lag in range(1, count):
            total = total + taps_ref[s, lag : lag + 1, :] * adj_ref[s, lag : lag + rows, :]
        outs[s][...] = total.astype(outs[s].dtype)
        tail_ref[s] = total[rows - TAIL : rows]
        for lag in range(count):
            window = pad_ref[s, RIM - lag : RIM - lag + rows, :]
            row = s * count + lag
            grads_ref[row : row + 1, :] = jnp.sum(adjoints[s] * window, axis=0, keepdims=True)
    base = 3 * count
    grads_ref[base : base + poles, :] = acc
    grads_ref[base + poles : base + poles + 1, :] = jnp.sum(z * p, axis=0, keepdims=True)


def tile(shape, lanes):
    nd = len(shape)
    return pl.BlockSpec(tuple(shape[:-1]) + (lanes,), lambda i: (0,) * (nd - 1) + (i,))


def run_states(q, k, v, c, rim, taps, a):
    rows, width = q.shape
    poles = a.shape[0]
    lanes = min(LANES, width)
    ins = (q, k, v, c, rim, taps, a)
    return pl.pallas_call(
        states_kernel,
        grid=(width // lanes,),
        in_specs=[tile(x.shape, lanes) for x in ins],
        out_specs=[tile((poles, width), lanes), tile((poles, width), lanes)],
        out_shape=[jax.ShapeDtypeStruct((poles, width), F32)] * 2,
        scratch_shapes=[
            pltpu.VMEM((3, rows + RIM, lanes), F32),
            pltpu.VMEM((rows, lanes), F32),
            pltpu.VMEM((rows, lanes), F32),
        ],
    )(*ins)


def run_main(q, k, v, c, rim, taps, a, r, skip, s_in, g_in):
    rows, width = q.shape
    poles = a.shape[0]
    count = taps.shape[1]
    lanes = min(LANES, width)
    ins = (q, k, v, c, rim, taps, a, r, skip, s_in, g_in)
    out_shapes = [
        jax.ShapeDtypeStruct((rows, width), jnp.bfloat16),
        jax.ShapeDtypeStruct((rows, width), jnp.bfloat16),
        jax.ShapeDtypeStruct((rows, width), jnp.bfloat16),
        jax.ShapeDtypeStruct((rows, width), jnp.bfloat16),
        jax.ShapeDtypeStruct((3, TAIL, width), F32),
        jax.ShapeDtypeStruct((3, RIM, width), F32),
        jax.ShapeDtypeStruct((3 * count + poles + 1, width), F32),
    ]
    return pl.pallas_call(
        main_kernel,
        grid=(width // lanes,),
        in_specs=[tile(x.shape, lanes) for x in ins],
        out_specs=[tile(o.shape, lanes) for o in out_shapes],
        out_shape=out_shapes,
        scratch_shapes=[
            pltpu.VMEM((3, rows + RIM, lanes), F32),
            pltpu.VMEM((rows, lanes), F32),
            pltpu.VMEM((rows, lanes), F32),
            pltpu.VMEM((rows, lanes), F32),
            pltpu.VMEM((rows, lanes), F32),
            pltpu.VMEM((3, rows + RIM, lanes), F32),
        ],
    )(*ins)


def exchange(x, axis, size):
    count = lax.axis_size(axis)
    return lax.ppermute(x, axis, [(i, i ^ size) for i in range(count)])


def decayed(decay, rows, steps):
    return jnp.exp(-decay * (rows * steps).astype(F32))


def scan_states(final_f, final_b, decay, rows, axis):
    count = lax.axis_size(axis)
    mine = lax.axis_index(axis)
    block_f, block_b = (final_f, final_b)
    incoming_f = jnp.zeros_like(final_f)
    incoming_b = jnp.zeros_like(final_b)
    levels = count.bit_length() - 1
    for level in range(levels):
        size = 1 << level
        upper = (mine // size) % 2 == 1
        pos = mine % size
        if level == levels - 1:
            got = exchange(jnp.where(upper, block_b, block_f), axis, size)
            got_f, got_b = (got, got)
        else:
            got = exchange(jnp.stack([block_f, block_b]), axis, size)
            got_f, got_b = (got[0], got[1])
        incoming_f = incoming_f + jnp.where(upper, decayed(decay, rows, pos) * got_f, 0.0)
        incoming_b = incoming_b + jnp.where(upper, 0.0, decayed(decay, rows, size - 1 - pos) * got_b)
        if level < levels - 1:
            jump = jnp.exp(-decay * float(rows * size))
            block_f = jnp.where(upper, block_f + jump * got_f, got_f + jump * block_f)
            block_b = jnp.where(upper, got_b + jump * block_b, block_b + jump * got_b)
    return (incoming_f, incoming_b)


def butterfly_sum(x, steps):
    shape = x.shape
    flat = x.reshape(-1)
    pieces = 1 << len(steps)
    unit = pieces * 128
    padded = -(-flat.shape[0] // unit) * unit
    flat = jnp.pad(flat, (0, padded - flat.shape[0])).reshape(-1, 128)
    sides = []
    for axis, size in steps:
        upper = (lax.axis_index(axis) // size) % 2 == 1
        sides.append(upper)
        half = flat.shape[0] // 2
        low, high = (flat[:half], flat[half:])
        keep = jnp.where(upper, high, low)
        send = jnp.where(upper, low, high)
        flat = keep + exchange(send, axis, size)
    for (axis, size), upper in reversed(list(zip(steps, sides))):
        got = exchange(flat, axis, size)
        flat = jnp.where(upper, jnp.concatenate([got, flat]), jnp.concatenate([flat, got]))
    return flat.reshape(-1)[: x.size].reshape(shape)


def sum_steps():
    steps = []
    dp_count = lax.axis_size("dp")
    seq_count = lax.axis_size("seq")
    if dp_count & (dp_count - 1) or seq_count & (seq_count - 1):
        return None
    dp_bits = [1 << b for b in range(dp_count.bit_length() - 1)]
    seq_bits = [1 << b for b in range(seq_count.bit_length() - 1)]
    steps = [("dp", size) for size in dp_bits[:1]]
    steps += [("seq", size) for size in seq_bits]
    steps += [("dp", size) for size in dp_bits[1:]]
    return steps


def per_device(queries, keys, values, cotangent, taps, residue, skip, decay):
    rows = queries.shape[1]
    width = queries.shape[2]
    count = taps.shape[1]
    poles = decay.shape[0]
    q, k, v, c = queries[0], keys[0], values[0], cotangent[0]
    rim = passed_along(jnp.stack([q[rows - RIM :], k[rows - RIM :], v[rows - RIM :]], 0), "seq", 1)
    a = jnp.exp(-decay)
    f_local, b_local = run_states(q, k, v, c, rim, taps, a)
    with jax.named_scope("modal_state_scan"):
        s_in, g_in = scan_states(f_local, b_local, decay, rows, "seq")
    mixed, gq, gk, gv, tails, heads, grads = run_main(
        q, k, v, c, rim, taps, a, residue, skip.reshape(1, width), s_in, g_in
    )
    after = passed_along(heads, "seq", -1)
    ext = jnp.concatenate(
        [jnp.zeros((3, TAIL, width), F32), after[:, : count - 1], jnp.zeros((3, 1, width), F32)], 1
    )
    corr = sum(taps[:, lag, None, :] * ext[:, lag : lag + TAIL] for lag in range(count))
    fixed = (tails + corr).astype(jnp.bfloat16)
    streams = [
        lax.dynamic_update_slice(g, fixed[idx], (rows - TAIL, 0)) for idx, g in enumerate((gq, gk, gv))
    ]
    steps = sum_steps()
    if steps is None:
        totals = lax.psum(grads, ("seq", "dp"))
    else:
        with jax.named_scope("filter_grad_sum"):
            totals = butterfly_sum(grads, steps)
    grad_taps = totals[: 3 * count].reshape(3, count, width)
    grad_residue = totals[3 * count : 3 * count + poles]
    grad_skip = totals[3 * count + poles]
    return (
        mixed[None],
        streams[0][None],
        streams[1][None],
        streams[2][None],
        grad_taps,
        grad_residue,
        grad_skip,
    )


def solution(mesh):
    return jax.shard_map(
        per_device,
        mesh=mesh,
        in_specs=(
            P("dp", "seq", None),
            P("dp", "seq", None),
            P("dp", "seq", None),
            P("dp", "seq", None),
            P(),
            P(),
            P(),
            P(),
        ),
        out_specs=(
            P("dp", "seq", None),
            P("dp", "seq", None),
            P("dp", "seq", None),
            P("dp", "seq", None),
            P(),
            P(),
            P(),
        ),
        check_vma=False,
    )
```

```python
import functools

import jax
import jax.numpy as jnp
from jax import lax
from jax.experimental import pallas as pl
from jax.experimental.pallas import tpu as pltpu
from jax.sharding import PartitionSpec as P

LANES = 512
RIM = 8
TAIL = 16
F32 = jnp.float32


def passed_along(x, axis, by):
    count = lax.axis_size(axis)
    pairs = [(i, i + by) for i in range(count) if 0 <= i + by < count]
    return lax.ppermute(x, axis, pairs)


def load_padded(x_ref, rim_ref, pad_ref, s):
    rows = x_ref.shape[0]
    pad_ref[s, 0:RIM, :] = rim_ref[s].astype(F32)
    pad_ref[s, RIM : RIM + rows, :] = x_ref[...].astype(F32)


def featurize(pad_ref, taps_ref, s, rows):
    count = taps_ref.shape[1]
    total = taps_ref[s, 0:1, :] * pad_ref[s, RIM : RIM + rows, :]
    for lag in range(1, count):
        total = total + taps_ref[s, lag : lag + 1, :] * pad_ref[s, RIM - lag : RIM - lag + rows, :]
    return total


def states_kernel(q_ref, k_ref, v_ref, c_ref, rim_ref, taps_ref, a_ref, f_ref, b_ref, pad_ref, p_ref, z_ref):
    rows = q_ref.shape[0]
    for s, x_ref in enumerate((q_ref, k_ref, v_ref)):
        load_padded(x_ref, rim_ref, pad_ref, s)
    fq = featurize(pad_ref, taps_ref, 0, rows)
    fk = featurize(pad_ref, taps_ref, 1, rows)
    fv = featurize(pad_ref, taps_ref, 2, rows)
    p_ref[...] = fk * fv
    z_ref[...] = c_ref[...].astype(F32) * fq
    a = a_ref[...]

    def step(i, carry):
        h, g = carry
        h = a * h + p_ref[pl.ds(i, 1), :]
        g = a * g + z_ref[pl.ds(rows - 1 - i, 1), :]
        return (h, g)

    zero = jnp.zeros_like(a)
    h, g = lax.fori_loop(0, rows, step, (zero, zero), unroll=8)
    f_ref[...] = h
    b_ref[...] = g


def main_kernel(
    q_ref, k_ref, v_ref, c_ref, rim_ref, taps_ref, a_ref, r_ref, skip_ref, s_ref, g_ref,
    mixed_ref, gq_ref, gk_ref, gv_ref, tail_ref, head_ref, grads_ref,
    pad_ref, p_ref, z_ref, y_ref, u_ref, adj_ref,
):
    rows = q_ref.shape[0]
    count = taps_ref.shape[1]
    poles = a_ref.shape[0]
    for s, x_ref in enumerate((q_ref, k_ref, v_ref)):
        load_padded(x_ref, rim_ref, pad_ref, s)
    fq = featurize(pad_ref, taps_ref, 0, rows)
    fk = featurize(pad_ref, taps_ref, 1, rows)
    fv = featurize(pad_ref, taps_ref, 2, rows)
    cot = c_ref[...].astype(F32)
    p_ref[...] = fk * fv
    z_ref[...] = cot * fq
    a = a_ref[...]
    r = r_ref[...]

    def step(i, carry):
        h, g, acc = carry
        h = a * h + p_ref[pl.ds(i, 1), :]
        acc = acc + z_ref[pl.ds(i, 1), :] * h
        y_ref[pl.ds(i, 1), :] = jnp.sum(r * h, axis=0, keepdims=True)
        back = rows - 1 - i
        g = a * g + z_ref[pl.ds(back, 1), :]
        u_ref[pl.ds(back, 1), :] = jnp.sum(r * g, axis=0, keepdims=True)
        return (h, g, acc)

    h, g, acc = lax.fori_loop(
        0, rows, step, (s_ref[...], g_ref[...], jnp.zeros_like(a)), unroll=8
    )
    skip = skip_ref[...]
    p = p_ref[...]
    z = z_ref[...]
    conv = y_ref[...] + skip * p
    mixed_ref[...] = (fq * conv).astype(mixed_ref.dtype)
    adj_u = u_ref[...] + skip * z
    adjoints = (cot * conv, adj_u * fv, adj_u * fk)
    zeros_rim = jnp.zeros((RIM, adj_ref.shape[2]), F32)
    outs = (gq_ref, gk_ref, gv_ref)
    for s in range(3):
        adj_ref[s, 0:rows, :] = adjoints[s]
        adj_ref[s, rows : rows + RIM, :] = zeros_rim
        head_ref[s] = adjoints[s][0:RIM]
        total = taps_ref[s, 0:1, :] * adjoints[s]
        for lag in range(1, count):
            total = total + taps_ref[s, lag : lag + 1, :] * adj_ref[s, lag : lag + rows, :]
        outs[s][...] = total.astype(outs[s].dtype)
        tail_ref[s] = total[rows - TAIL : rows]
        for lag in range(count):
            window = pad_ref[s, RIM - lag : RIM - lag + rows, :]
            row = s * count + lag
            grads_ref[row : row + 1, :] = jnp.sum(adjoints[s] * window, axis=0, keepdims=True)
    base = 3 * count
    grads_ref[base : base + poles, :] = acc
    grads_ref[base + poles : base + poles + 1, :] = jnp.sum(z * p, axis=0, keepdims=True)


def tile(shape, lanes):
    nd = len(shape)
    return pl.BlockSpec(tuple(shape[:-1]) + (lanes,), lambda i: (0,) * (nd - 1) + (i,))


def run_states(q, k, v, c, rim, taps, a):
    rows, width = q.shape
    poles = a.shape[0]
    lanes = min(LANES, width)
    ins = (q, k, v, c, rim, taps, a)
    return pl.pallas_call(
        states_kernel,
        grid=(width // lanes,),
        in_specs=[tile(x.shape, lanes) for x in ins],
        out_specs=[tile((poles, width), lanes), tile((poles, width), lanes)],
        out_shape=[jax.ShapeDtypeStruct((poles, width), F32)] * 2,
        scratch_shapes=[
            pltpu.VMEM((3, rows + RIM, lanes), F32),
            pltpu.VMEM((rows, lanes), F32),
            pltpu.VMEM((rows, lanes), F32),
        ],
    )(*ins)


def run_main(q, k, v, c, rim, taps, a, r, skip, s_in, g_in):
    rows, width = q.shape
    poles = a.shape[0]
    count = taps.shape[1]
    lanes = min(LANES, width)
    ins = (q, k, v, c, rim, taps, a, r, skip, s_in, g_in)
    out_shapes = [
        jax.ShapeDtypeStruct((rows, width), jnp.bfloat16),
        jax.ShapeDtypeStruct((rows, width), jnp.bfloat16),
        jax.ShapeDtypeStruct((rows, width), jnp.bfloat16),
        jax.ShapeDtypeStruct((rows, width), jnp.bfloat16),
        jax.ShapeDtypeStruct((3, TAIL, width), F32),
        jax.ShapeDtypeStruct((3, RIM, width), F32),
        jax.ShapeDtypeStruct((3 * count + poles + 1, width), F32),
    ]
    return pl.pallas_call(
        main_kernel,
        grid=(width // lanes,),
        in_specs=[tile(x.shape, lanes) for x in ins],
        out_specs=[tile(o.shape, lanes) for o in out_shapes],
        out_shape=out_shapes,
        scratch_shapes=[
            pltpu.VMEM((3, rows + RIM, lanes), F32),
            pltpu.VMEM((rows, lanes), F32),
            pltpu.VMEM((rows, lanes), F32),
            pltpu.VMEM((rows, lanes), F32),
            pltpu.VMEM((rows, lanes), F32),
            pltpu.VMEM((3, rows + RIM, lanes), F32),
        ],
    )(*ins)


def exchange(x, axis, size):
    count = lax.axis_size(axis)
    return lax.ppermute(x, axis, [(i, i ^ size) for i in range(count)])


def decayed(decay, rows, steps):
    return jnp.exp(-decay * (rows * steps).astype(F32))


def scan_states(final_f, final_b, decay, rows, axis):
    count = lax.axis_size(axis)
    mine = lax.axis_index(axis)
    block_f, block_b = (final_f, final_b)
    incoming_f = jnp.zeros_like(final_f)
    incoming_b = jnp.zeros_like(final_b)
    levels = count.bit_length() - 1
    for level in range(levels):
        size = 1 << level
        upper = (mine // size) % 2 == 1
        pos = mine % size
        if level == levels - 1:
            got = exchange(jnp.where(upper, block_b, block_f), axis, size)
            got_f, got_b = (got, got)
        else:
            got = exchange(jnp.stack([block_f, block_b]), axis, size)
            got_f, got_b = (got[0], got[1])
        incoming_f = incoming_f + jnp.where(upper, decayed(decay, rows, pos) * got_f, 0.0)
        incoming_b = incoming_b + jnp.where(upper, 0.0, decayed(decay, rows, size - 1 - pos) * got_b)
        if level < levels - 1:
            jump = jnp.exp(-decay * float(rows * size))
            block_f = jnp.where(upper, block_f + jump * got_f, got_f + jump * block_f)
            block_b = jnp.where(upper, got_b + jump * block_b, block_b + jump * got_b)
    return (incoming_f, incoming_b)


def butterfly_sum(x, steps):
    shape = x.shape
    flat = x.reshape(-1)
    pieces = 1 << len(steps)
    unit = pieces * 128
    padded = -(-flat.shape[0] // unit) * unit
    flat = jnp.pad(flat, (0, padded - flat.shape[0])).reshape(-1, 128)
    sides = []
    for axis, size in steps:
        upper = (lax.axis_index(axis) // size) % 2 == 1
        sides.append(upper)
        half = flat.shape[0] // 2
        low, high = (flat[:half], flat[half:])
        keep = jnp.where(upper, high, low)
        send = jnp.where(upper, low, high)
        flat = keep + exchange(send, axis, size)
    for (axis, size), upper in reversed(list(zip(steps, sides))):
        got = exchange(flat, axis, size)
        flat = jnp.where(upper, jnp.concatenate([got, flat]), jnp.concatenate([flat, got]))
    return flat.reshape(-1)[: x.size].reshape(shape)


def sum_steps():
    steps = []
    dp_count = lax.axis_size("dp")
    seq_count = lax.axis_size("seq")
    if dp_count & (dp_count - 1) or seq_count & (seq_count - 1):
        return None
    dp_bits = [1 << b for b in range(dp_count.bit_length() - 1)]
    seq_bits = [1 << b for b in range(seq_count.bit_length() - 1)]
    steps = [("dp", size) for size in dp_bits[:1]]
    steps += [("seq", size) for size in seq_bits]
    steps += [("dp", size) for size in dp_bits[1:]]
    return steps


def per_device(queries, keys, values, cotangent, taps, residue, skip, decay):
    rows = queries.shape[1]
    width = queries.shape[2]
    count = taps.shape[1]
    poles = decay.shape[0]
    q, k, v, c = queries[0], keys[0], values[0], cotangent[0]
    lead = jnp.stack([q[rows - RIM :], k[rows - RIM :], v[rows - RIM :]], 0)
    rim = passed_along(lead, "seq", 1)
    a = jnp.exp(-decay)
    f_bare, b_bare = run_states(q, k, v, c, jnp.zeros_like(lead), taps, a)
    with jax.named_scope("rim_share_of_states"):
        first = jnp.stack([q[:RIM], k[:RIM], v[:RIM]], 0).astype(F32)

        def head_feats(before):
            padded = jnp.concatenate([before, first], 1)
            return sum(taps[:, lag, None, :] * padded[:, RIM - lag : 2 * RIM - lag] for lag in range(count))

        with_rim = head_feats(rim.astype(F32))
        without = head_feats(jnp.zeros_like(first))
        d_product = with_rim[1] * with_rim[2] - without[1] * without[2]
        d_adjoint = c[:RIM].astype(F32) * (with_rim[0] - without[0])
        lags = jnp.arange(RIM, dtype=F32)
        f_local = f_bare + jnp.sum(
            jnp.exp(-decay[None] * (rows - 1 - lags)[:, None, None]) * d_product[:, None, :], 0
        )
        b_local = b_bare + jnp.sum(jnp.exp(-decay[None] * lags[:, None, None]) * d_adjoint[:, None, :], 0)
    with jax.named_scope("modal_state_scan"):
        s_in, g_in = scan_states(f_local, b_local, decay, rows, "seq")
    mixed, gq, gk, gv, tails, heads, grads = run_main(
        q, k, v, c, rim, taps, a, residue, skip.reshape(1, width), s_in, g_in
    )
    after = passed_along(heads, "seq", -1)
    ext = jnp.concatenate(
        [jnp.zeros((3, TAIL, width), F32), after[:, : count - 1], jnp.zeros((3, 1, width), F32)], 1
    )
    corr = sum(taps[:, lag, None, :] * ext[:, lag : lag + TAIL] for lag in range(count))
    fixed = (tails + corr).astype(jnp.bfloat16)
    streams = [
        lax.dynamic_update_slice(g, fixed[idx], (rows - TAIL, 0)) for idx, g in enumerate((gq, gk, gv))
    ]
    steps = sum_steps()
    if steps is None:
        totals = lax.psum(grads, ("seq", "dp"))
    else:
        with jax.named_scope("filter_grad_sum"):
            totals = butterfly_sum(grads, steps)
    grad_taps = totals[: 3 * count].reshape(3, count, width)
    grad_residue = totals[3 * count : 3 * count + poles]
    grad_skip = totals[3 * count + poles]
    return (
        mixed[None],
        streams[0][None],
        streams[1][None],
        streams[2][None],
        grad_taps,
        grad_residue,
        grad_skip,
    )


def solution(mesh):
    return jax.shard_map(
        per_device,
        mesh=mesh,
        in_specs=(
            P("dp", "seq", None),
            P("dp", "seq", None),
            P("dp", "seq", None),
            P("dp", "seq", None),
            P(),
            P(),
            P(),
            P(),
        ),
        out_specs=(
            P("dp", "seq", None),
            P("dp", "seq", None),
            P("dp", "seq", None),
            P("dp", "seq", None),
            P(),
            P(),
            P(),
        ),
        check_vma=False,
    )
```

```python
import functools

import jax
import jax.numpy as jnp
from jax import lax
from jax.experimental import pallas as pl
from jax.experimental.pallas import tpu as pltpu
from jax.sharding import PartitionSpec as P

LANES = 512
RIM = 8
TAIL = 16
BR = 16
F32 = jnp.float32


def passed_along(x, axis, by):
    count = lax.axis_size(axis)
    pairs = [(i, i + by) for i in range(count) if 0 <= i + by < count]
    return lax.ppermute(x, axis, pairs)


def fill_rows(x_refs, pad_ref, lo):
    for s, x_ref in enumerate(x_refs):
        pad_ref[s, RIM + lo : RIM + lo + BR, :] = x_ref[lo : lo + BR, :].astype(F32)


def block_feature(pad_ref, taps_ref, s, lo):
    count = taps_ref.shape[1]
    total = taps_ref[s, 0:1, :] * pad_ref[s, RIM + lo : RIM + lo + BR, :]
    for lag in range(1, count):
        total = total + taps_ref[s, lag : lag + 1, :] * pad_ref[s, RIM + lo - lag : RIM + lo - lag + BR, :]
    return total


def states_kernel(q_ref, k_ref, v_ref, c_ref, rim_ref, taps_ref, a_ref, f_ref, b_ref, pad_ref, p_ref, z_ref):
    rows = q_ref.shape[0]
    for s in range(3):
        pad_ref[s, 0:RIM, :] = rim_ref[s].astype(F32)
    for lo in range(0, rows, BR):
        fill_rows((q_ref, k_ref, v_ref), pad_ref, lo)
        fq = block_feature(pad_ref, taps_ref, 0, lo)
        fk = block_feature(pad_ref, taps_ref, 1, lo)
        fv = block_feature(pad_ref, taps_ref, 2, lo)
        p_ref[lo : lo + BR, :] = fk * fv
        z_ref[lo : lo + BR, :] = c_ref[lo : lo + BR, :].astype(F32) * fq
    a = a_ref[...]

    def step(i, carry):
        h, g = carry
        h = a * h + p_ref[pl.ds(i, 1), :]
        g = a * g + z_ref[pl.ds(rows - 1 - i, 1), :]
        return (h, g)

    zero = jnp.zeros_like(a)
    h, g = lax.fori_loop(0, rows, step, (zero, zero), unroll=8)
    f_ref[...] = h
    b_ref[...] = g


def fold(x):
    return x[0:8] + x[8:16]


def main_kernel(
    q_ref, k_ref, v_ref, c_ref, rim_ref, taps_ref, a_ref, r_ref, skip_ref, s_ref, g_ref,
    mixed_ref, gq_ref, gk_ref, gv_ref, tail_ref, head_ref, grads_ref,
    pad_ref, p_ref, z_ref, y_ref, u_ref, adj_ref, feat_ref,
):
    rows = q_ref.shape[0]
    count = taps_ref.shape[1]
    poles = a_ref.shape[0]
    lanes = q_ref.shape[1]
    for s in range(3):
        pad_ref[s, 0:RIM, :] = rim_ref[s].astype(F32)
    skip_sum = jnp.zeros((8, lanes), F32)
    for lo in range(0, rows, BR):
        fill_rows((q_ref, k_ref, v_ref), pad_ref, lo)
        fq = block_feature(pad_ref, taps_ref, 0, lo)
        fk = block_feature(pad_ref, taps_ref, 1, lo)
        fv = block_feature(pad_ref, taps_ref, 2, lo)
        feat_ref[0, lo : lo + BR, :] = fq
        feat_ref[1, lo : lo + BR, :] = fk
        feat_ref[2, lo : lo + BR, :] = fv
        p = fk * fv
        z = c_ref[lo : lo + BR, :].astype(F32) * fq
        p_ref[lo : lo + BR, :] = p
        z_ref[lo : lo + BR, :] = z
        skip_sum = skip_sum + fold(z * p)
    a = a_ref[...]
    r = r_ref[...]

    def step(i, carry):
        h, g, acc = carry
        h = a * h + p_ref[pl.ds(i, 1), :]
        acc = acc + z_ref[pl.ds(i, 1), :] * h
        y_ref[pl.ds(i, 1), :] = jnp.sum(r * h, axis=0, keepdims=True)
        back = rows - 1 - i
        g = a * g + z_ref[pl.ds(back, 1), :]
        u_ref[pl.ds(back, 1), :] = jnp.sum(r * g, axis=0, keepdims=True)
        return (h, g, acc)

    h, g, acc = lax.fori_loop(
        0, rows, step, (s_ref[...], g_ref[...], jnp.zeros_like(a)), unroll=8
    )
    skip = skip_ref[...]
    for lo in range(0, rows, BR):
        fq = feat_ref[0, lo : lo + BR, :]
        conv = y_ref[lo : lo + BR, :] + skip * p_ref[lo : lo + BR, :]
        mixed_ref[lo : lo + BR, :] = (fq * conv).astype(mixed_ref.dtype)
        adj_u = u_ref[lo : lo + BR, :] + skip * z_ref[lo : lo + BR, :]
        adj_ref[0, lo : lo + BR, :] = c_ref[lo : lo + BR, :].astype(F32) * conv
        adj_ref[1, lo : lo + BR, :] = adj_u * feat_ref[2, lo : lo + BR, :]
        adj_ref[2, lo : lo + BR, :] = adj_u * feat_ref[1, lo : lo + BR, :]
    zeros_rim = jnp.zeros((RIM, lanes), F32)
    outs = (gq_ref, gk_ref, gv_ref)
    for s in range(3):
        adj_ref[s, rows : rows + RIM, :] = zeros_rim
        head_ref[s] = adj_ref[s, 0:RIM, :]
        sums = [jnp.zeros((8, lanes), F32) for _ in range(count)]
        for lo in range(0, rows, BR):
            x = pad_ref[s, RIM + lo : RIM + lo + BR, :]
            total = None
            for lag in range(count):
                window = adj_ref[s, lo + lag : lo + lag + BR, :]
                term = taps_ref[s, lag : lag + 1, :] * window
                total = term if total is None else total + term
                sums[lag] = sums[lag] + fold(window * x)
            outs[s][lo : lo + BR, :] = total.astype(outs[s].dtype)
            if lo + BR == rows:
                tail_ref[s] = total[BR - TAIL :]
        for lag in range(count):
            value = jnp.sum(sums[lag], axis=0, keepdims=True)
            if lag > 0:
                edge = adj_ref[s, 0:lag, :] * pad_ref[s, RIM - lag : RIM, :]
                value = value + jnp.sum(edge, axis=0, keepdims=True)
            row = s * count + lag
            grads_ref[row : row + 1, :] = value
    base = 3 * count
    grads_ref[base : base + poles, :] = acc
    grads_ref[base + poles : base + poles + 1, :] = jnp.sum(skip_sum, axis=0, keepdims=True)


def tile(shape, lanes):
    nd = len(shape)
    return pl.BlockSpec(tuple(shape[:-1]) + (lanes,), lambda i: (0,) * (nd - 1) + (i,))


def run_states(q, k, v, c, rim, taps, a):
    rows, width = q.shape
    poles = a.shape[0]
    lanes = min(LANES, width)
    ins = (q, k, v, c, rim, taps, a)
    return pl.pallas_call(
        states_kernel,
        grid=(width // lanes,),
        in_specs=[tile(x.shape, lanes) for x in ins],
        out_specs=[tile((poles, width), lanes), tile((poles, width), lanes)],
        out_shape=[jax.ShapeDtypeStruct((poles, width), F32)] * 2,
        scratch_shapes=[
            pltpu.VMEM((3, rows + RIM, lanes), F32),
            pltpu.VMEM((rows, lanes), F32),
            pltpu.VMEM((rows, lanes), F32),
        ],
    )(*ins)


def run_main(q, k, v, c, rim, taps, a, r, skip, s_in, g_in):
    rows, width = q.shape
    poles = a.shape[0]
    count = taps.shape[1]
    lanes = min(LANES, width)
    ins = (q, k, v, c, rim, taps, a, r, skip, s_in, g_in)
    out_shapes = [
        jax.ShapeDtypeStruct((rows, width), jnp.bfloat16),
        jax.ShapeDtypeStruct((rows, width), jnp.bfloat16),
        jax.ShapeDtypeStruct((rows, width), jnp.bfloat16),
        jax.ShapeDtypeStruct((rows, width), jnp.bfloat16),
        jax.ShapeDtypeStruct((3, TAIL, width), F32),
        jax.ShapeDtypeStruct((3, RIM, width), F32),
        jax.ShapeDtypeStruct((3 * count + poles + 1, width), F32),
    ]
    return pl.pallas_call(
        main_kernel,
        grid=(width // lanes,),
        in_specs=[tile(x.shape, lanes) for x in ins],
        out_specs=[tile(o.shape, lanes) for o in out_shapes],
        out_shape=out_shapes,
        scratch_shapes=[
            pltpu.VMEM((3, rows + RIM, lanes), F32),
            pltpu.VMEM((rows, lanes), F32),
            pltpu.VMEM((rows, lanes), F32),
            pltpu.VMEM((rows, lanes), F32),
            pltpu.VMEM((rows, lanes), F32),
            pltpu.VMEM((3, rows + RIM, lanes), F32),
            pltpu.VMEM((3, rows, lanes), F32),
        ],
    )(*ins)


def exchange(x, axis, size):
    count = lax.axis_size(axis)
    return lax.ppermute(x, axis, [(i, i ^ size) for i in range(count)])


def decayed(decay, rows, steps):
    return jnp.exp(-decay * (rows * steps).astype(F32))


def scan_states(final_f, final_b, decay, rows, axis):
    count = lax.axis_size(axis)
    mine = lax.axis_index(axis)
    block_f, block_b = (final_f, final_b)
    incoming_f = jnp.zeros_like(final_f)
    incoming_b = jnp.zeros_like(final_b)
    levels = count.bit_length() - 1
    for level in range(levels):
        size = 1 << level
        upper = (mine // size) % 2 == 1
        pos = mine % size
        if level == levels - 1:
            got = exchange(jnp.where(upper, block_b, block_f), axis, size)
            got_f, got_b = (got, got)
        else:
            got = exchange(jnp.stack([block_f, block_b]), axis, size)
            got_f, got_b = (got[0], got[1])
        incoming_f = incoming_f + jnp.where(upper, decayed(decay, rows, pos) * got_f, 0.0)
        incoming_b = incoming_b + jnp.where(upper, 0.0, decayed(decay, rows, size - 1 - pos) * got_b)
        if level < levels - 1:
            jump = jnp.exp(-decay * float(rows * size))
            block_f = jnp.where(upper, block_f + jump * got_f, got_f + jump * block_f)
            block_b = jnp.where(upper, got_b + jump * block_b, block_b + jump * got_b)
    return (incoming_f, incoming_b)


def butterfly_sum(x, steps):
    shape = x.shape
    flat = x.reshape(-1)
    pieces = 1 << len(steps)
    unit = pieces * 128
    padded = -(-flat.shape[0] // unit) * unit
    flat = jnp.pad(flat, (0, padded - flat.shape[0])).reshape(-1, 128)
    sides = []
    for axis, size in steps:
        upper = (lax.axis_index(axis) // size) % 2 == 1
        sides.append(upper)
        half = flat.shape[0] // 2
        low, high = (flat[:half], flat[half:])
        keep = jnp.where(upper, high, low)
        send = jnp.where(upper, low, high)
        flat = keep + exchange(send, axis, size)
    for (axis, size), upper in reversed(list(zip(steps, sides))):
        got = exchange(flat, axis, size)
        flat = jnp.where(upper, jnp.concatenate([got, flat]), jnp.concatenate([flat, got]))
    return flat.reshape(-1)[: x.size].reshape(shape)


def sum_steps():
    steps = []
    dp_count = lax.axis_size("dp")
    seq_count = lax.axis_size("seq")
    if dp_count & (dp_count - 1) or seq_count & (seq_count - 1):
        return None
    dp_bits = [1 << b for b in range(dp_count.bit_length() - 1)]
    seq_bits = [1 << b for b in range(seq_count.bit_length() - 1)]
    steps = [("dp", size) for size in dp_bits[:1]]
    steps += [("seq", size) for size in seq_bits]
    steps += [("dp", size) for size in dp_bits[1:]]
    return steps


def per_device(queries, keys, values, cotangent, taps, residue, skip, decay):
    rows = queries.shape[1]
    width = queries.shape[2]
    count = taps.shape[1]
    poles = decay.shape[0]
    q, k, v, c = queries[0], keys[0], values[0], cotangent[0]
    lead = jnp.stack([q[rows - RIM :], k[rows - RIM :], v[rows - RIM :]], 0)
    rim = passed_along(lead, "seq", 1)
    a = jnp.exp(-decay)
    f_bare, b_bare = run_states(q, k, v, c, jnp.zeros_like(lead), taps, a)
    with jax.named_scope("rim_share_of_states"):
        first = jnp.stack([q[:RIM], k[:RIM], v[:RIM]], 0).astype(F32)

        def head_feats(before):
            padded = jnp.concatenate([before, first], 1)
            return sum(taps[:, lag, None, :] * padded[:, RIM - lag : 2 * RIM - lag] for lag in range(count))

        with_rim = head_feats(rim.astype(F32))
        without = head_feats(jnp.zeros_like(first))
        d_product = with_rim[1] * with_rim[2] - without[1] * without[2]
        d_adjoint = c[:RIM].astype(F32) * (with_rim[0] - without[0])
        lags = jnp.arange(RIM, dtype=F32)
        f_local = f_bare + jnp.sum(
            jnp.exp(-decay[None] * (rows - 1 - lags)[:, None, None]) * d_product[:, None, :], 0
        )
        b_local = b_bare + jnp.sum(jnp.exp(-decay[None] * lags[:, None, None]) * d_adjoint[:, None, :], 0)
    with jax.named_scope("modal_state_scan"):
        s_in, g_in = scan_states(f_local, b_local, decay, rows, "seq")
    mixed, gq, gk, gv, tails, heads, grads = run_main(
        q, k, v, c, rim, taps, a, residue, skip.reshape(1, width), s_in, g_in
    )
    after = passed_along(heads, "seq", -1)
    ext = jnp.concatenate(
        [jnp.zeros((3, TAIL, width), F32), after[:, : count - 1], jnp.zeros((3, 1, width), F32)], 1
    )
    corr = sum(taps[:, lag, None, :] * ext[:, lag : lag + TAIL] for lag in range(count))
    fixed = (tails + corr).astype(jnp.bfloat16)
    streams = [
        lax.dynamic_update_slice(g, fixed[idx], (rows - TAIL, 0)) for idx, g in enumerate((gq, gk, gv))
    ]
    steps = sum_steps()
    if steps is None:
        totals = lax.psum(grads, ("seq", "dp"))
    else:
        with jax.named_scope("filter_grad_sum"):
            totals = butterfly_sum(grads, steps)
    grad_taps = totals[: 3 * count].reshape(3, count, width)
    grad_residue = totals[3 * count : 3 * count + poles]
    grad_skip = totals[3 * count + poles]
    return (
        mixed[None],
        streams[0][None],
        streams[1][None],
        streams[2][None],
        grad_taps,
        grad_residue,
        grad_skip,
    )


def solution(mesh):
    return jax.shard_map(
        per_device,
        mesh=mesh,
        in_specs=(
            P("dp", "seq", None),
            P("dp", "seq", None),
            P("dp", "seq", None),
            P("dp", "seq", None),
            P(),
            P(),
            P(),
            P(),
        ),
        out_specs=(
            P("dp", "seq", None),
            P("dp", "seq", None),
            P("dp", "seq", None),
            P("dp", "seq", None),
            P(),
            P(),
            P(),
        ),
        check_vma=False,
    )
```

```python
import functools

import jax
import jax.numpy as jnp
from jax import lax
from jax.experimental import pallas as pl
from jax.experimental.pallas import tpu as pltpu
from jax.sharding import PartitionSpec as P

LANES = 512
RIM = 8
TAIL = 16
BR = 16
F32 = jnp.float32


def passed_along(x, axis, by):
    count = lax.axis_size(axis)
    pairs = [(i, i + by) for i in range(count) if 0 <= i + by < count]
    return lax.ppermute(x, axis, pairs)


def fill_rows(x_refs, pad_ref, lo):
    for s, x_ref in enumerate(x_refs):
        pad_ref[s, RIM + lo : RIM + lo + BR, :] = x_ref[lo : lo + BR, :].astype(F32)


def block_feature(pad_ref, taps_ref, s, lo):
    count = taps_ref.shape[1]
    total = taps_ref[s, 0:1, :] * pad_ref[s, RIM + lo : RIM + lo + BR, :]
    for lag in range(1, count):
        total = total + taps_ref[s, lag : lag + 1, :] * pad_ref[s, RIM + lo - lag : RIM + lo - lag + BR, :]
    return total


def states_kernel(q_ref, k_ref, v_ref, c_ref, rim_ref, taps_ref, a_ref, f_ref, b_ref, pad_ref, p_ref, z_ref):
    rows = q_ref.shape[0]
    for s in range(3):
        pad_ref[s, 0:RIM, :] = rim_ref[s].astype(F32)
    for lo in range(0, rows, BR):
        fill_rows((q_ref, k_ref, v_ref), pad_ref, lo)
        fq = block_feature(pad_ref, taps_ref, 0, lo)
        fk = block_feature(pad_ref, taps_ref, 1, lo)
        fv = block_feature(pad_ref, taps_ref, 2, lo)
        p_ref[lo : lo + BR, :] = fk * fv
        z_ref[lo : lo + BR, :] = c_ref[lo : lo + BR, :].astype(F32) * fq
    a = a_ref[...]

    def step(i, carry):
        h, g = carry
        h = a * h + p_ref[pl.ds(i, 1), :]
        g = a * g + z_ref[pl.ds(rows - 1 - i, 1), :]
        return (h, g)

    zero = jnp.zeros_like(a)
    h, g = lax.fori_loop(0, rows, step, (zero, zero), unroll=8)
    f_ref[...] = h
    b_ref[...] = g


def fold(x):
    return x[0:8] + x[8:16]


def main_kernel(
    q_ref, k_ref, v_ref, c_ref, rim_ref, taps_ref, a_ref, r_ref, skip_ref, s_ref, g_ref,
    mixed_ref, gq_ref, gk_ref, gv_ref, tail_ref, head_ref, grads_ref,
    pad_ref, p_ref, z_ref, y_ref, u_ref, adj_ref, feat_ref,
):
    rows = q_ref.shape[0]
    count = taps_ref.shape[1]
    poles = a_ref.shape[0]
    lanes = q_ref.shape[1]
    for s in range(3):
        pad_ref[s, 0:RIM, :] = rim_ref[s].astype(F32)
    skip_sum = jnp.zeros((8, lanes), F32)
    for lo in range(0, rows, BR):
        fill_rows((q_ref, k_ref, v_ref), pad_ref, lo)
        fq = block_feature(pad_ref, taps_ref, 0, lo)
        fk = block_feature(pad_ref, taps_ref, 1, lo)
        fv = block_feature(pad_ref, taps_ref, 2, lo)
        feat_ref[0, lo : lo + BR, :] = fq
        feat_ref[1, lo : lo + BR, :] = fk
        feat_ref[2, lo : lo + BR, :] = fv
        p = fk * fv
        z = c_ref[lo : lo + BR, :].astype(F32) * fq
        p_ref[lo : lo + BR, :] = p
        z_ref[lo : lo + BR, :] = z
        skip_sum = skip_sum + fold(z * p)
    a = a_ref[...]
    r = r_ref[...]

    def step(i, carry):
        h, g, acc = carry
        h = a * h + p_ref[pl.ds(i, 1), :]
        acc = acc + z_ref[pl.ds(i, 1), :] * h
        y_ref[pl.ds(i, 1), :] = jnp.sum(r * h, axis=0, keepdims=True)
        back = rows - 1 - i
        g = a * g + z_ref[pl.ds(back, 1), :]
        u_ref[pl.ds(back, 1), :] = jnp.sum(r * g, axis=0, keepdims=True)
        return (h, g, acc)

    h, g, acc = lax.fori_loop(
        0, rows, step, (s_ref[...], g_ref[...], jnp.zeros_like(a)), unroll=8
    )
    skip = skip_ref[...]
    for lo in range(0, rows, BR):
        fq = feat_ref[0, lo : lo + BR, :]
        conv = y_ref[lo : lo + BR, :] + skip * p_ref[lo : lo + BR, :]
        mixed_ref[lo : lo + BR, :] = (fq * conv).astype(mixed_ref.dtype)
        adj_u = u_ref[lo : lo + BR, :] + skip * z_ref[lo : lo + BR, :]
        adj_ref[0, lo : lo + BR, :] = c_ref[lo : lo + BR, :].astype(F32) * conv
        adj_ref[1, lo : lo + BR, :] = adj_u * feat_ref[2, lo : lo + BR, :]
        adj_ref[2, lo : lo + BR, :] = adj_u * feat_ref[1, lo : lo + BR, :]
    zeros_rim = jnp.zeros((RIM, lanes), F32)
    outs = (gq_ref, gk_ref, gv_ref)
    for s in range(3):
        adj_ref[s, rows : rows + RIM, :] = zeros_rim
        head_ref[s] = adj_ref[s, 0:RIM, :]
        sums = [jnp.zeros((8, lanes), F32) for _ in range(count)]
        for lo in range(0, rows, BR):
            x = pad_ref[s, RIM + lo : RIM + lo + BR, :]
            total = None
            for lag in range(count):
                window = adj_ref[s, lo + lag : lo + lag + BR, :]
                term = taps_ref[s, lag : lag + 1, :] * window
                total = term if total is None else total + term
                sums[lag] = sums[lag] + fold(window * x)
            outs[s][lo : lo + BR, :] = total.astype(outs[s].dtype)
            if lo + BR == rows:
                tail_ref[s] = total[BR - TAIL :]
        for lag in range(count):
            value = jnp.sum(sums[lag], axis=0, keepdims=True)
            if lag > 0:
                edge = adj_ref[s, 0:lag, :] * pad_ref[s, RIM - lag : RIM, :]
                value = value + jnp.sum(edge, axis=0, keepdims=True)
            row = s * count + lag
            grads_ref[row : row + 1, :] = value
    base = 3 * count
    grads_ref[base : base + poles, :] = acc
    grads_ref[base + poles : base + poles + 1, :] = jnp.sum(skip_sum, axis=0, keepdims=True)


def tile(shape, lanes):
    nd = len(shape)
    return pl.BlockSpec(tuple(shape[:-1]) + (lanes,), lambda i: (0,) * (nd - 1) + (i,))


def run_states(q, k, v, c, rim, taps, a):
    rows, width = q.shape
    poles = a.shape[0]
    lanes = min(LANES, width)
    ins = (q, k, v, c, rim, taps, a)
    return pl.pallas_call(
        states_kernel,
        grid=(width // lanes,),
        in_specs=[tile(x.shape, lanes) for x in ins],
        out_specs=[tile((poles, width), lanes), tile((poles, width), lanes)],
        out_shape=[jax.ShapeDtypeStruct((poles, width), F32)] * 2,
        scratch_shapes=[
            pltpu.VMEM((3, rows + RIM, lanes), F32),
            pltpu.VMEM((rows, lanes), F32),
            pltpu.VMEM((rows, lanes), F32),
        ],
    )(*ins)


def run_main(q, k, v, c, rim, taps, a, r, skip, s_in, g_in):
    rows, width = q.shape
    poles = a.shape[0]
    count = taps.shape[1]
    lanes = min(LANES, width)
    ins = (q, k, v, c, rim, taps, a, r, skip, s_in, g_in)
    out_shapes = [
        jax.ShapeDtypeStruct((rows, width), jnp.bfloat16),
        jax.ShapeDtypeStruct((rows, width), jnp.bfloat16),
        jax.ShapeDtypeStruct((rows, width), jnp.bfloat16),
        jax.ShapeDtypeStruct((rows, width), jnp.bfloat16),
        jax.ShapeDtypeStruct((3, TAIL, width), F32),
        jax.ShapeDtypeStruct((3, RIM, width), F32),
        jax.ShapeDtypeStruct((3 * count + poles + 1, width), F32),
    ]
    return pl.pallas_call(
        main_kernel,
        grid=(width // lanes,),
        in_specs=[tile(x.shape, lanes) for x in ins],
        out_specs=[tile(o.shape, lanes) for o in out_shapes],
        out_shape=out_shapes,
        scratch_shapes=[
            pltpu.VMEM((3, rows + RIM, lanes), F32),
            pltpu.VMEM((rows, lanes), F32),
            pltpu.VMEM((rows, lanes), F32),
            pltpu.VMEM((rows, lanes), F32),
            pltpu.VMEM((rows, lanes), F32),
            pltpu.VMEM((3, rows + RIM, lanes), F32),
            pltpu.VMEM((3, rows, lanes), F32),
        ],
    )(*ins)


def exchange(x, axis, size):
    count = lax.axis_size(axis)
    return lax.ppermute(x, axis, [(i, i ^ size) for i in range(count)])


def decayed(decay, rows, steps):
    return jnp.exp(-decay * (rows * steps).astype(F32))


def scan_states(final_f, final_b, decay, rows, axis):
    count = lax.axis_size(axis)
    mine = lax.axis_index(axis)
    block_f, block_b = (final_f, final_b)
    incoming_f = jnp.zeros_like(final_f)
    incoming_b = jnp.zeros_like(final_b)
    levels = count.bit_length() - 1
    for level in range(levels):
        size = 1 << level
        upper = (mine // size) % 2 == 1
        pos = mine % size
        if level == levels - 1:
            sent = jnp.where(upper, block_b, block_f)
            half = sent.shape[1] // 2
            got = jnp.concatenate(
                [exchange(sent[:, :half], axis, size), exchange(sent[:, half:], axis, size)], 1
            )
            got_f, got_b = (got, got)
        else:
            got_f = exchange(block_f, axis, size)
            got_b = exchange(block_b, axis, size)
        incoming_f = incoming_f + jnp.where(upper, decayed(decay, rows, pos) * got_f, 0.0)
        incoming_b = incoming_b + jnp.where(upper, 0.0, decayed(decay, rows, size - 1 - pos) * got_b)
        if level < levels - 1:
            jump = jnp.exp(-decay * float(rows * size))
            block_f = jnp.where(upper, block_f + jump * got_f, got_f + jump * block_f)
            block_b = jnp.where(upper, got_b + jump * block_b, block_b + jump * got_b)
    return (incoming_f, incoming_b)


def butterfly_sum(x, steps):
    shape = x.shape
    flat = x.reshape(-1)
    pieces = 1 << len(steps)
    unit = pieces * 128
    padded = -(-flat.shape[0] // unit) * unit
    flat = jnp.pad(flat, (0, padded - flat.shape[0])).reshape(-1, 128)
    sides = []
    for axis, size in steps:
        upper = (lax.axis_index(axis) // size) % 2 == 1
        sides.append(upper)
        half = flat.shape[0] // 2
        low, high = (flat[:half], flat[half:])
        keep = jnp.where(upper, high, low)
        send = jnp.where(upper, low, high)
        flat = keep + exchange(send, axis, size)
    for (axis, size), upper in reversed(list(zip(steps, sides))):
        got = exchange(flat, axis, size)
        flat = jnp.where(upper, jnp.concatenate([got, flat]), jnp.concatenate([flat, got]))
    return flat.reshape(-1)[: x.size].reshape(shape)


def sum_steps():
    steps = []
    dp_count = lax.axis_size("dp")
    seq_count = lax.axis_size("seq")
    if dp_count & (dp_count - 1) or seq_count & (seq_count - 1):
        return None
    dp_bits = [1 << b for b in range(dp_count.bit_length() - 1)]
    seq_bits = [1 << b for b in range(seq_count.bit_length() - 1)]
    steps = [("dp", size) for size in dp_bits[:1]]
    steps += [("seq", size) for size in seq_bits]
    steps += [("dp", size) for size in dp_bits[1:]]
    return steps


def per_device(queries, keys, values, cotangent, taps, residue, skip, decay):
    rows = queries.shape[1]
    width = queries.shape[2]
    count = taps.shape[1]
    poles = decay.shape[0]
    q, k, v, c = queries[0], keys[0], values[0], cotangent[0]
    lead = jnp.stack([q[rows - RIM :], k[rows - RIM :], v[rows - RIM :]], 0)
    rim = passed_along(lead, "seq", 1)
    a = jnp.exp(-decay)
    f_bare, b_bare = run_states(q, k, v, c, jnp.zeros_like(lead), taps, a)
    with jax.named_scope("rim_share_of_states"):
        first = jnp.stack([q[:RIM], k[:RIM], v[:RIM]], 0).astype(F32)

        def head_feats(before):
            padded = jnp.concatenate([before, first], 1)
            return sum(taps[:, lag, None, :] * padded[:, RIM - lag : 2 * RIM - lag] for lag in range(count))

        with_rim = head_feats(rim.astype(F32))
        without = head_feats(jnp.zeros_like(first))
        d_product = with_rim[1] * with_rim[2] - without[1] * without[2]
        d_adjoint = c[:RIM].astype(F32) * (with_rim[0] - without[0])
        lags = jnp.arange(RIM, dtype=F32)
        f_local = f_bare + jnp.sum(
            jnp.exp(-decay[None] * (rows - 1 - lags)[:, None, None]) * d_product[:, None, :], 0
        )
        b_local = b_bare + jnp.sum(jnp.exp(-decay[None] * lags[:, None, None]) * d_adjoint[:, None, :], 0)
    with jax.named_scope("modal_state_scan"):
        s_in, g_in = scan_states(f_local, b_local, decay, rows, "seq")
    mixed, gq, gk, gv, tails, heads, grads = run_main(
        q, k, v, c, rim, taps, a, residue, skip.reshape(1, width), s_in, g_in
    )
    after = passed_along(heads, "seq", -1)
    ext = jnp.concatenate(
        [jnp.zeros((3, TAIL, width), F32), after[:, : count - 1], jnp.zeros((3, 1, width), F32)], 1
    )
    corr = sum(taps[:, lag, None, :] * ext[:, lag : lag + TAIL] for lag in range(count))
    fixed = (tails + corr).astype(jnp.bfloat16)
    streams = [
        lax.dynamic_update_slice(g, fixed[idx], (rows - TAIL, 0)) for idx, g in enumerate((gq, gk, gv))
    ]
    steps = sum_steps()
    if steps is None:
        totals = lax.psum(grads, ("seq", "dp"))
    else:
        with jax.named_scope("filter_grad_sum"):
            totals = butterfly_sum(grads, steps)
    grad_taps = totals[: 3 * count].reshape(3, count, width)
    grad_residue = totals[3 * count : 3 * count + poles]
    grad_skip = totals[3 * count + poles]
    return (
        mixed[None],
        streams[0][None],
        streams[1][None],
        streams[2][None],
        grad_taps,
        grad_residue,
        grad_skip,
    )


def solution(mesh):
    return jax.shard_map(
        per_device,
        mesh=mesh,
        in_specs=(
            P("dp", "seq", None),
            P("dp", "seq", None),
            P("dp", "seq", None),
            P("dp", "seq", None),
            P(),
            P(),
            P(),
            P(),
        ),
        out_specs=(
            P("dp", "seq", None),
            P("dp", "seq", None),
            P("dp", "seq", None),
            P("dp", "seq", None),
            P(),
            P(),
            P(),
        ),
        check_vma=False,
    )
```

```python
import functools

import jax
import jax.numpy as jnp
from jax import lax
from jax.experimental import pallas as pl
from jax.experimental.pallas import tpu as pltpu
from jax.sharding import PartitionSpec as P

LANES = 512
RIM = 8
TAIL = 16
BR = 16
F32 = jnp.float32


def passed_along(x, axis, by):
    count = lax.axis_size(axis)
    pairs = [(i, i + by) for i in range(count) if 0 <= i + by < count]
    return lax.ppermute(x, axis, pairs)


CHUNK = 256


def sublanes(lanes):
    return lax.broadcasted_iota(jnp.int32, (8, lanes), 0)


def feature_stream(pad_ref, taps_ref, s, out_ref):
    rows = out_ref.shape[1]
    count = taps_ref.shape[1]
    for c0 in range(0, out_ref.shape[2], CHUNK):
        cols = slice(c0, c0 + CHUNK)
        sub = sublanes(CHUNK)
        taps = [taps_ref[s, lag : lag + 1, cols] for lag in range(count)]
        prev = [pltpu.roll(pad_ref[s, 0:8, cols], lag, 0) for lag in range(1, count)]
        for i in range(rows // 8):
            cur = pad_ref[s, 8 * (i + 1) : 8 * (i + 2), cols]
            total = taps[0] * cur
            rolled = []
            for lag in range(1, count):
                turned = pltpu.roll(cur, lag, 0)
                total = total + taps[lag] * jnp.where(sub < lag, prev[lag - 1], turned)
                rolled.append(turned)
            prev = rolled
            out_ref[s, 8 * i : 8 * (i + 1), cols] = total


def fill_rows(x_refs, pad_ref, lo):
    for s, x_ref in enumerate(x_refs):
        pad_ref[s, RIM + lo : RIM + lo + BR, :] = x_ref[lo : lo + BR, :].astype(F32)


def block_feature(pad_ref, taps_ref, s, lo):
    count = taps_ref.shape[1]
    total = taps_ref[s, 0:1, :] * pad_ref[s, RIM + lo : RIM + lo + BR, :]
    for lag in range(1, count):
        total = total + taps_ref[s, lag : lag + 1, :] * pad_ref[s, RIM + lo - lag : RIM + lo - lag + BR, :]
    return total


def states_kernel(
    q_ref, k_ref, v_ref, c_ref, rim_ref, taps_ref, a_ref, f_ref, b_ref, pad_ref, p_ref, z_ref, feat_ref
):
    rows = q_ref.shape[0]
    for s in range(3):
        pad_ref[s, 0:RIM, :] = rim_ref[s].astype(F32)
    for lo in range(0, rows, BR):
        fill_rows((q_ref, k_ref, v_ref), pad_ref, lo)
    for s in range(3):
        feature_stream(pad_ref, taps_ref, s, feat_ref)
    for lo in range(0, rows, BR):
        p_ref[lo : lo + BR, :] = feat_ref[1, lo : lo + BR, :] * feat_ref[2, lo : lo + BR, :]
        z_ref[lo : lo + BR, :] = c_ref[lo : lo + BR, :].astype(F32) * feat_ref[0, lo : lo + BR, :]
    a = a_ref[...]

    def step(i, carry):
        h, g = carry
        h = a * h + p_ref[pl.ds(i, 1), :]
        g = a * g + z_ref[pl.ds(rows - 1 - i, 1), :]
        return (h, g)

    zero = jnp.zeros_like(a)
    h, g = lax.fori_loop(0, rows, step, (zero, zero), unroll=8)
    f_ref[...] = h
    b_ref[...] = g


def fold(x):
    return x[0:8] + x[8:16]


def main_kernel(
    q_ref, k_ref, v_ref, c_ref, rim_ref, taps_ref, a_ref, r_ref, skip_ref, s_ref, g_ref,
    mixed_ref, gq_ref, gk_ref, gv_ref, tail_ref, head_ref, grads_ref,
    pad_ref, p_ref, z_ref, y_ref, u_ref, adj_ref, feat_ref,
):
    rows = q_ref.shape[0]
    count = taps_ref.shape[1]
    poles = a_ref.shape[0]
    lanes = q_ref.shape[1]
    for s in range(3):
        pad_ref[s, 0:RIM, :] = rim_ref[s].astype(F32)
    skip_sum = jnp.zeros((8, lanes), F32)
    for lo in range(0, rows, BR):
        fill_rows((q_ref, k_ref, v_ref), pad_ref, lo)
    for s in range(3):
        feature_stream(pad_ref, taps_ref, s, feat_ref)
    for lo in range(0, rows, BR):
        fq = feat_ref[0, lo : lo + BR, :]
        fk = feat_ref[1, lo : lo + BR, :]
        fv = feat_ref[2, lo : lo + BR, :]
        p = fk * fv
        z = c_ref[lo : lo + BR, :].astype(F32) * fq
        p_ref[lo : lo + BR, :] = p
        z_ref[lo : lo + BR, :] = z
        skip_sum = skip_sum + fold(z * p)
    a = a_ref[...]
    r = r_ref[...]

    def step(i, carry):
        h, g, acc = carry
        h = a * h + p_ref[pl.ds(i, 1), :]
        acc = acc + z_ref[pl.ds(i, 1), :] * h
        y_ref[pl.ds(i, 1), :] = jnp.sum(r * h, axis=0, keepdims=True)
        back = rows - 1 - i
        g = a * g + z_ref[pl.ds(back, 1), :]
        u_ref[pl.ds(back, 1), :] = jnp.sum(r * g, axis=0, keepdims=True)
        return (h, g, acc)

    h, g, acc = lax.fori_loop(
        0, rows, step, (s_ref[...], g_ref[...], jnp.zeros_like(a)), unroll=8
    )
    skip = skip_ref[...]
    for lo in range(0, rows, BR):
        fq = feat_ref[0, lo : lo + BR, :]
        conv = y_ref[lo : lo + BR, :] + skip * p_ref[lo : lo + BR, :]
        mixed_ref[lo : lo + BR, :] = (fq * conv).astype(mixed_ref.dtype)
        adj_u = u_ref[lo : lo + BR, :] + skip * z_ref[lo : lo + BR, :]
        adj_ref[0, lo : lo + BR, :] = c_ref[lo : lo + BR, :].astype(F32) * conv
        adj_ref[1, lo : lo + BR, :] = adj_u * feat_ref[2, lo : lo + BR, :]
        adj_ref[2, lo : lo + BR, :] = adj_u * feat_ref[1, lo : lo + BR, :]
    zeros_rim = jnp.zeros((RIM, lanes), F32)
    outs = (gq_ref, gk_ref, gv_ref)
    for s in range(3):
        adj_ref[s, rows : rows + RIM, :] = zeros_rim
        head_ref[s] = adj_ref[s, 0:RIM, :]
    for s in range(3):
        for c0 in range(0, lanes, CHUNK):
            cols = slice(c0, c0 + CHUNK)
            sub = sublanes(CHUNK)
            taps = [taps_ref[s, lag : lag + 1, cols] for lag in range(count)]
            sums = [jnp.zeros((8, CHUNK), F32) for _ in range(count)]
            prev = [pltpu.roll(adj_ref[s, 0:8, cols], 8 - lag, 0) for lag in range(1, count)]
            done = []
            for i in range(rows // 8):
                cur = adj_ref[s, 8 * i : 8 * (i + 1), cols]
                after = adj_ref[s, 8 * (i + 1) : 8 * (i + 2), cols]
                x = pad_ref[s, RIM + 8 * i : RIM + 8 * (i + 1), cols]
                total = taps[0] * cur
                sums[0] = sums[0] + cur * x
                rolled = []
                for lag in range(1, count):
                    turned = pltpu.roll(after, 8 - lag, 0)
                    window = jnp.where(sub < 8 - lag, prev[lag - 1], turned)
                    total = total + taps[lag] * window
                    sums[lag] = sums[lag] + window * x
                    rolled.append(turned)
                prev = rolled
                done.append(total)
                if len(done) == 2:
                    both = jnp.concatenate(done, 0)
                    lo = 8 * (i - 1)
                    outs[s][lo : lo + BR, cols] = both.astype(outs[s].dtype)
                    if lo + BR == rows:
                        tail_ref[s, :, cols] = both[BR - TAIL :]
                    done = []
            for lag in range(count):
                value = jnp.sum(sums[lag], axis=0, keepdims=True)
                if lag > 0:
                    edge = adj_ref[s, 0:lag, cols] * pad_ref[s, RIM - lag : RIM, cols]
                    value = value + jnp.sum(edge, axis=0, keepdims=True)
                row = s * count + lag
                grads_ref[row : row + 1, cols] = value
    base = 3 * count
    grads_ref[base : base + poles, :] = acc
    grads_ref[base + poles : base + poles + 1, :] = jnp.sum(skip_sum, axis=0, keepdims=True)


def tile(shape, lanes):
    nd = len(shape)
    return pl.BlockSpec(tuple(shape[:-1]) + (lanes,), lambda i: (0,) * (nd - 1) + (i,))


def run_states(q, k, v, c, rim, taps, a):
    rows, width = q.shape
    poles = a.shape[0]
    lanes = min(LANES, width)
    ins = (q, k, v, c, rim, taps, a)
    return pl.pallas_call(
        states_kernel,
        grid=(width // lanes,),
        in_specs=[tile(x.shape, lanes) for x in ins],
        out_specs=[tile((poles, width), lanes), tile((poles, width), lanes)],
        out_shape=[jax.ShapeDtypeStruct((poles, width), F32)] * 2,
        scratch_shapes=[
            pltpu.VMEM((3, rows + RIM, lanes), F32),
            pltpu.VMEM((rows, lanes), F32),
            pltpu.VMEM((rows, lanes), F32),
            pltpu.VMEM((3, rows, lanes), F32),
        ],
    )(*ins)


def run_main(q, k, v, c, rim, taps, a, r, skip, s_in, g_in):
    rows, width = q.shape
    poles = a.shape[0]
    count = taps.shape[1]
    lanes = min(LANES, width)
    ins = (q, k, v, c, rim, taps, a, r, skip, s_in, g_in)
    out_shapes = [
        jax.ShapeDtypeStruct((rows, width), jnp.bfloat16),
        jax.ShapeDtypeStruct((rows, width), jnp.bfloat16),
        jax.ShapeDtypeStruct((rows, width), jnp.bfloat16),
        jax.ShapeDtypeStruct((rows, width), jnp.bfloat16),
        jax.ShapeDtypeStruct((3, TAIL, width), F32),
        jax.ShapeDtypeStruct((3, RIM, width), F32),
        jax.ShapeDtypeStruct((3 * count + poles + 1, width), F32),
    ]
    return pl.pallas_call(
        main_kernel,
        grid=(width // lanes,),
        in_specs=[tile(x.shape, lanes) for x in ins],
        out_specs=[tile(o.shape, lanes) for o in out_shapes],
        out_shape=out_shapes,
        scratch_shapes=[
            pltpu.VMEM((3, rows + RIM, lanes), F32),
            pltpu.VMEM((rows, lanes), F32),
            pltpu.VMEM((rows, lanes), F32),
            pltpu.VMEM((rows, lanes), F32),
            pltpu.VMEM((rows, lanes), F32),
            pltpu.VMEM((3, rows + RIM, lanes), F32),
            pltpu.VMEM((3, rows, lanes), F32),
        ],
    )(*ins)


def exchange(x, axis, size):
    count = lax.axis_size(axis)
    return lax.ppermute(x, axis, [(i, i ^ size) for i in range(count)])


def decayed(decay, rows, steps):
    return jnp.exp(-decay * (rows * steps).astype(F32))


def scan_states(final_f, final_b, decay, rows, axis):
    count = lax.axis_size(axis)
    mine = lax.axis_index(axis)
    block_f, block_b = (final_f, final_b)
    incoming_f = jnp.zeros_like(final_f)
    incoming_b = jnp.zeros_like(final_b)
    levels = count.bit_length() - 1
    for level in range(levels):
        size = 1 << level
        upper = (mine // size) % 2 == 1
        pos = mine % size
        if level == levels - 1:
            sent = jnp.where(upper, block_b, block_f)
            half = sent.shape[1] // 2
            got = jnp.concatenate(
                [exchange(sent[:, :half], axis, size), exchange(sent[:, half:], axis, size)], 1
            )
            got_f, got_b = (got, got)
        else:
            got_f = exchange(block_f, axis, size)
            got_b = exchange(block_b, axis, size)
        incoming_f = incoming_f + jnp.where(upper, decayed(decay, rows, pos) * got_f, 0.0)
        incoming_b = incoming_b + jnp.where(upper, 0.0, decayed(decay, rows, size - 1 - pos) * got_b)
        if level < levels - 1:
            jump = jnp.exp(-decay * float(rows * size))
            block_f = jnp.where(upper, block_f + jump * got_f, got_f + jump * block_f)
            block_b = jnp.where(upper, got_b + jump * block_b, block_b + jump * got_b)
    return (incoming_f, incoming_b)


def butterfly_sum(x, steps):
    shape = x.shape
    flat = x.reshape(-1)
    pieces = 1 << len(steps)
    unit = pieces * 128
    padded = -(-flat.shape[0] // unit) * unit
    flat = jnp.pad(flat, (0, padded - flat.shape[0])).reshape(-1, 128)
    sides = []
    for axis, size in steps:
        upper = (lax.axis_index(axis) // size) % 2 == 1
        sides.append(upper)
        half = flat.shape[0] // 2
        low, high = (flat[:half], flat[half:])
        keep = jnp.where(upper, high, low)
        send = jnp.where(upper, low, high)
        flat = keep + exchange(send, axis, size)
    for (axis, size), upper in reversed(list(zip(steps, sides))):
        got = exchange(flat, axis, size)
        flat = jnp.where(upper, jnp.concatenate([got, flat]), jnp.concatenate([flat, got]))
    return flat.reshape(-1)[: x.size].reshape(shape)


def sum_steps():
    steps = []
    dp_count = lax.axis_size("dp")
    seq_count = lax.axis_size("seq")
    if dp_count & (dp_count - 1) or seq_count & (seq_count - 1):
        return None
    dp_bits = [1 << b for b in range(dp_count.bit_length() - 1)]
    seq_bits = [1 << b for b in range(seq_count.bit_length() - 1)]
    steps = [("dp", size) for size in dp_bits[:1]]
    steps += [("seq", size) for size in seq_bits]
    steps += [("dp", size) for size in dp_bits[1:]]
    return steps


def per_device(queries, keys, values, cotangent, taps, residue, skip, decay):
    rows = queries.shape[1]
    width = queries.shape[2]
    count = taps.shape[1]
    poles = decay.shape[0]
    q, k, v, c = queries[0], keys[0], values[0], cotangent[0]
    lead = jnp.stack([q[rows - RIM :], k[rows - RIM :], v[rows - RIM :]], 0)
    rim = passed_along(lead, "seq", 1)
    a = jnp.exp(-decay)
    f_bare, b_bare = run_states(q, k, v, c, jnp.zeros_like(lead), taps, a)
    with jax.named_scope("rim_share_of_states"):
        first = jnp.stack([q[:RIM], k[:RIM], v[:RIM]], 0).astype(F32)

        def head_feats(before):
            padded = jnp.concatenate([before, first], 1)
            return sum(taps[:, lag, None, :] * padded[:, RIM - lag : 2 * RIM - lag] for lag in range(count))

        with_rim = head_feats(rim.astype(F32))
        without = head_feats(jnp.zeros_like(first))
        d_product = with_rim[1] * with_rim[2] - without[1] * without[2]
        d_adjoint = c[:RIM].astype(F32) * (with_rim[0] - without[0])
        lags = jnp.arange(RIM, dtype=F32)
        f_local = f_bare + jnp.sum(
            jnp.exp(-decay[None] * (rows - 1 - lags)[:, None, None]) * d_product[:, None, :], 0
        )
        b_local = b_bare + jnp.sum(jnp.exp(-decay[None] * lags[:, None, None]) * d_adjoint[:, None, :], 0)
    with jax.named_scope("modal_state_scan"):
        s_in, g_in = scan_states(f_local, b_local, decay, rows, "seq")
    mixed, gq, gk, gv, tails, heads, grads = run_main(
        q, k, v, c, rim, taps, a, residue, skip.reshape(1, width), s_in, g_in
    )
    after = passed_along(heads, "seq", -1)
    ext = jnp.concatenate(
        [jnp.zeros((3, TAIL, width), F32), after[:, : count - 1], jnp.zeros((3, 1, width), F32)], 1
    )
    corr = sum(taps[:, lag, None, :] * ext[:, lag : lag + TAIL] for lag in range(count))
    fixed = (tails + corr).astype(jnp.bfloat16)
    streams = [
        lax.dynamic_update_slice(g, fixed[idx], (rows - TAIL, 0)) for idx, g in enumerate((gq, gk, gv))
    ]
    steps = sum_steps()
    if steps is None:
        totals = lax.psum(grads, ("seq", "dp"))
    else:
        with jax.named_scope("filter_grad_sum"):
            totals = butterfly_sum(grads, steps)
    grad_taps = totals[: 3 * count].reshape(3, count, width)
    grad_residue = totals[3 * count : 3 * count + poles]
    grad_skip = totals[3 * count + poles]
    return (
        mixed[None],
        streams[0][None],
        streams[1][None],
        streams[2][None],
        grad_taps,
        grad_residue,
        grad_skip,
    )


def solution(mesh):
    return jax.shard_map(
        per_device,
        mesh=mesh,
        in_specs=(
            P("dp", "seq", None),
            P("dp", "seq", None),
            P("dp", "seq", None),
            P("dp", "seq", None),
            P(),
            P(),
            P(),
            P(),
        ),
        out_specs=(
            P("dp", "seq", None),
            P("dp", "seq", None),
            P("dp", "seq", None),
            P("dp", "seq", None),
            P(),
            P(),
            P(),
        ),
        check_vma=False,
    )
```

```python
import functools

import jax
import jax.numpy as jnp
from jax import lax
from jax.experimental import pallas as pl
from jax.experimental.pallas import tpu as pltpu
from jax.sharding import PartitionSpec as P

LANES = 512
RIM = 8
TAIL = 16
BR = 16
F32 = jnp.float32


def passed_along(x, axis, by):
    count = lax.axis_size(axis)
    pairs = [(i, i + by) for i in range(count) if 0 <= i + by < count]
    return lax.ppermute(x, axis, pairs)


CHUNK = 256


def sublanes(lanes):
    return lax.broadcasted_iota(jnp.int32, (8, lanes), 0)


def feature_stream(pad_ref, taps_ref, s, out_ref):
    rows = out_ref.shape[1]
    count = taps_ref.shape[1]
    for c0 in range(0, out_ref.shape[2], CHUNK):
        cols = slice(c0, c0 + CHUNK)
        sub = sublanes(CHUNK)
        taps = [taps_ref[s, lag : lag + 1, cols] for lag in range(count)]
        prev = [pltpu.roll(pad_ref[s, 0:8, cols], lag, 0) for lag in range(1, count)]
        for i in range(rows // 8):
            cur = pad_ref[s, 8 * (i + 1) : 8 * (i + 2), cols]
            total = taps[0] * cur
            rolled = []
            for lag in range(1, count):
                turned = pltpu.roll(cur, lag, 0)
                total = total + taps[lag] * jnp.where(sub < lag, prev[lag - 1], turned)
                rolled.append(turned)
            prev = rolled
            out_ref[s, 8 * i : 8 * (i + 1), cols] = total


def fill_rows(x_refs, pad_ref, lo):
    for s, x_ref in enumerate(x_refs):
        pad_ref[s, RIM + lo : RIM + lo + BR, :] = x_ref[lo : lo + BR, :].astype(F32)


def block_feature(pad_ref, taps_ref, s, lo):
    count = taps_ref.shape[1]
    total = taps_ref[s, 0:1, :] * pad_ref[s, RIM + lo : RIM + lo + BR, :]
    for lag in range(1, count):
        total = total + taps_ref[s, lag : lag + 1, :] * pad_ref[s, RIM + lo - lag : RIM + lo - lag + BR, :]
    return total


def states_kernel(
    q_ref, k_ref, v_ref, c_ref, rim_ref, taps_ref, a_ref, f_ref, b_ref, pad_ref, p_ref, z_ref, feat_ref
):
    rows = q_ref.shape[0]
    for s in range(3):
        pad_ref[s, 0:RIM, :] = rim_ref[s].astype(F32)
    for lo in range(0, rows, BR):
        fill_rows((q_ref, k_ref, v_ref), pad_ref, lo)
    for s in range(3):
        feature_stream(pad_ref, taps_ref, s, feat_ref)
    for lo in range(0, rows, BR):
        p_ref[lo : lo + BR, :] = feat_ref[1, lo : lo + BR, :] * feat_ref[2, lo : lo + BR, :]
        z_ref[lo : lo + BR, :] = c_ref[lo : lo + BR, :].astype(F32) * feat_ref[0, lo : lo + BR, :]
    a = a_ref[...]

    def step(i, carry):
        h, g = carry
        h = a * h + p_ref[pl.ds(i, 1), :]
        g = a * g + z_ref[pl.ds(rows - 1 - i, 1), :]
        return (h, g)

    zero = jnp.zeros_like(a)
    h, g = lax.fori_loop(0, rows, step, (zero, zero), unroll=8)
    f_ref[...] = h
    b_ref[...] = g


def fold(x):
    return x[0:8] + x[8:16]


def main_kernel(
    q_ref, k_ref, v_ref, c_ref, rim_ref, taps_ref, a_ref, r_ref, skip_ref, s_ref, g_ref,
    mixed_ref, gq_ref, gk_ref, gv_ref, tail_ref, head_ref, grads_ref,
    pad_ref, p_ref, z_ref, y_ref, u_ref, adj_ref, feat_ref,
):
    rows = q_ref.shape[0]
    count = taps_ref.shape[1]
    poles = a_ref.shape[0]
    lanes = q_ref.shape[1]
    for s in range(3):
        pad_ref[s, 0:RIM, :] = rim_ref[s].astype(F32)
    skip_sum = jnp.zeros((8, lanes), F32)
    for lo in range(0, rows, BR):
        fill_rows((q_ref, k_ref, v_ref), pad_ref, lo)
    for s in range(3):
        feature_stream(pad_ref, taps_ref, s, feat_ref)
    for lo in range(0, rows, BR):
        fq = feat_ref[0, lo : lo + BR, :]
        fk = feat_ref[1, lo : lo + BR, :]
        fv = feat_ref[2, lo : lo + BR, :]
        p = fk * fv
        z = c_ref[lo : lo + BR, :].astype(F32) * fq
        p_ref[lo : lo + BR, :] = p
        z_ref[lo : lo + BR, :] = z
        skip_sum = skip_sum + fold(z * p)
    a = a_ref[...]
    r = r_ref[...]

    def step(i, carry):
        h, g, acc = carry
        h = a * h + p_ref[pl.ds(i, 1), :]
        acc = acc + z_ref[pl.ds(i, 1), :] * h
        y_ref[pl.ds(i, 1), :] = jnp.sum(r * h, axis=0, keepdims=True)
        back = rows - 1 - i
        g = a * g + z_ref[pl.ds(back, 1), :]
        u_ref[pl.ds(back, 1), :] = jnp.sum(r * g, axis=0, keepdims=True)
        return (h, g, acc)

    h, g, acc = lax.fori_loop(
        0, rows, step, (s_ref[...], g_ref[...], jnp.zeros_like(a)), unroll=8
    )
    skip = skip_ref[...]
    for lo in range(0, rows, BR):
        fq = feat_ref[0, lo : lo + BR, :]
        conv = y_ref[lo : lo + BR, :] + skip * p_ref[lo : lo + BR, :]
        mixed_ref[lo : lo + BR, :] = (fq * conv).astype(mixed_ref.dtype)
        adj_u = u_ref[lo : lo + BR, :] + skip * z_ref[lo : lo + BR, :]
        adj_ref[0, lo : lo + BR, :] = c_ref[lo : lo + BR, :].astype(F32) * conv
        adj_ref[1, lo : lo + BR, :] = adj_u * feat_ref[2, lo : lo + BR, :]
        adj_ref[2, lo : lo + BR, :] = adj_u * feat_ref[1, lo : lo + BR, :]
    zeros_rim = jnp.zeros((RIM, lanes), F32)
    outs = (gq_ref, gk_ref, gv_ref)
    for s in range(3):
        adj_ref[s, rows : rows + RIM, :] = zeros_rim
        head_ref[s] = adj_ref[s, 0:RIM, :]
    for s in range(3):
        for c0 in range(0, lanes, CHUNK):
            cols = slice(c0, c0 + CHUNK)
            sub = sublanes(CHUNK)
            taps = [taps_ref[s, lag : lag + 1, cols] for lag in range(count)]
            sums = [jnp.zeros((8, CHUNK), F32) for _ in range(count)]
            prev = [pltpu.roll(adj_ref[s, 0:8, cols], 8 - lag, 0) for lag in range(1, count)]
            done = []
            for i in range(rows // 8):
                cur = adj_ref[s, 8 * i : 8 * (i + 1), cols]
                after = adj_ref[s, 8 * (i + 1) : 8 * (i + 2), cols]
                x = pad_ref[s, RIM + 8 * i : RIM + 8 * (i + 1), cols]
                total = taps[0] * cur
                sums[0] = sums[0] + cur * x
                rolled = []
                for lag in range(1, count):
                    turned = pltpu.roll(after, 8 - lag, 0)
                    window = jnp.where(sub < 8 - lag, prev[lag - 1], turned)
                    total = total + taps[lag] * window
                    sums[lag] = sums[lag] + window * x
                    rolled.append(turned)
                prev = rolled
                done.append(total)
                if len(done) == 2:
                    both = jnp.concatenate(done, 0)
                    lo = 8 * (i - 1)
                    outs[s][lo : lo + BR, cols] = both.astype(outs[s].dtype)
                    if lo + BR == rows:
                        tail_ref[s, :, cols] = both[BR - TAIL :]
                    done = []
            for lag in range(count):
                value = jnp.sum(sums[lag], axis=0, keepdims=True)
                if lag > 0:
                    edge = adj_ref[s, 0:lag, cols] * pad_ref[s, RIM - lag : RIM, cols]
                    value = value + jnp.sum(edge, axis=0, keepdims=True)
                row = s * count + lag
                grads_ref[row : row + 1, cols] = value
    base = 3 * count
    grads_ref[base : base + poles, :] = acc
    grads_ref[base + poles : base + poles + 1, :] = jnp.sum(skip_sum, axis=0, keepdims=True)


def tile(shape, lanes):
    nd = len(shape)
    return pl.BlockSpec(tuple(shape[:-1]) + (lanes,), lambda i: (0,) * (nd - 1) + (i,))


def run_states(q, k, v, c, rim, taps, a):
    rows, width = q.shape
    poles = a.shape[0]
    lanes = min(LANES, width)
    ins = (q, k, v, c, rim, taps, a)
    return pl.pallas_call(
        states_kernel,
        grid=(width // lanes,),
        in_specs=[tile(x.shape, lanes) for x in ins],
        out_specs=[tile((poles, width), lanes), tile((poles, width), lanes)],
        out_shape=[jax.ShapeDtypeStruct((poles, width), F32)] * 2,
        scratch_shapes=[
            pltpu.VMEM((3, rows + RIM, lanes), F32),
            pltpu.VMEM((rows, lanes), F32),
            pltpu.VMEM((rows, lanes), F32),
            pltpu.VMEM((3, rows, lanes), F32),
        ],
    )(*ins)


def run_main(q, k, v, c, rim, taps, a, r, skip, s_in, g_in):
    rows, width = q.shape
    poles = a.shape[0]
    count = taps.shape[1]
    lanes = min(LANES, width)
    ins = (q, k, v, c, rim, taps, a, r, skip, s_in, g_in)
    out_shapes = [
        jax.ShapeDtypeStruct((rows, width), jnp.bfloat16),
        jax.ShapeDtypeStruct((rows, width), jnp.bfloat16),
        jax.ShapeDtypeStruct((rows, width), jnp.bfloat16),
        jax.ShapeDtypeStruct((rows, width), jnp.bfloat16),
        jax.ShapeDtypeStruct((3, TAIL, width), F32),
        jax.ShapeDtypeStruct((3, RIM, width), F32),
        jax.ShapeDtypeStruct((3 * count + poles + 1, width), F32),
    ]
    return pl.pallas_call(
        main_kernel,
        grid=(width // lanes,),
        in_specs=[tile(x.shape, lanes) for x in ins],
        out_specs=[tile(o.shape, lanes) for o in out_shapes],
        out_shape=out_shapes,
        scratch_shapes=[
            pltpu.VMEM((3, rows + RIM, lanes), F32),
            pltpu.VMEM((rows, lanes), F32),
            pltpu.VMEM((rows, lanes), F32),
            pltpu.VMEM((rows, lanes), F32),
            pltpu.VMEM((rows, lanes), F32),
            pltpu.VMEM((3, rows + RIM, lanes), F32),
            pltpu.VMEM((3, rows, lanes), F32),
        ],
    )(*ins)


def exchange(x, axis, size):
    count = lax.axis_size(axis)
    return lax.ppermute(x, axis, [(i, i ^ size) for i in range(count)])


def decayed(decay, rows, steps):
    return jnp.exp(-decay * (rows * steps).astype(F32))


def scan_four(final_f, final_b, decay, rows, axis, mine):
    jump = jnp.exp(-decay * float(rows))
    got = exchange(jnp.where(mine % 2 == 1, final_b, final_f), axis, 1)
    pair_f = final_f + jump * got
    pair_b = final_b + jump * got
    sent = jnp.where(mine == 1, pair_f, pair_b)
    across = lax.ppermute(sent, axis, [(1, 3), (2, 0)])
    diagonal = lax.ppermute(sent, axis, [(1, 2), (2, 1)])
    zero = jnp.zeros_like(final_f)
    incoming_f = jnp.where(
        mine == 3, got + jump * across, jnp.where(mine == 2, diagonal, jnp.where(mine == 1, got, zero))
    )
    incoming_b = jnp.where(
        mine == 0, got + jump * across, jnp.where(mine == 1, diagonal, jnp.where(mine == 2, got, zero))
    )
    return (incoming_f, incoming_b)


def scan_states(final_f, final_b, decay, rows, axis):
    count = lax.axis_size(axis)
    mine = lax.axis_index(axis)
    if count == 4:
        return scan_four(final_f, final_b, decay, rows, axis, mine)
    block_f, block_b = (final_f, final_b)
    incoming_f = jnp.zeros_like(final_f)
    incoming_b = jnp.zeros_like(final_b)
    levels = count.bit_length() - 1
    for level in range(levels):
        size = 1 << level
        upper = (mine // size) % 2 == 1
        pos = mine % size
        if level == levels - 1:
            sent = jnp.where(upper, block_b, block_f)
            half = sent.shape[1] // 2
            got = jnp.concatenate(
                [exchange(sent[:, :half], axis, size), exchange(sent[:, half:], axis, size)], 1
            )
            got_f, got_b = (got, got)
        else:
            got_f = exchange(block_f, axis, size)
            got_b = exchange(block_b, axis, size)
        incoming_f = incoming_f + jnp.where(upper, decayed(decay, rows, pos) * got_f, 0.0)
        incoming_b = incoming_b + jnp.where(upper, 0.0, decayed(decay, rows, size - 1 - pos) * got_b)
        if level < levels - 1:
            jump = jnp.exp(-decay * float(rows * size))
            block_f = jnp.where(upper, block_f + jump * got_f, got_f + jump * block_f)
            block_b = jnp.where(upper, got_b + jump * block_b, block_b + jump * got_b)
    return (incoming_f, incoming_b)


def butterfly_sum(x, steps):
    shape = x.shape
    flat = x.reshape(-1)
    pieces = 1 << len(steps)
    unit = pieces * 128
    padded = -(-flat.shape[0] // unit) * unit
    flat = jnp.pad(flat, (0, padded - flat.shape[0])).reshape(-1, 128)
    sides = []
    for axis, size in steps:
        upper = (lax.axis_index(axis) // size) % 2 == 1
        sides.append(upper)
        half = flat.shape[0] // 2
        low, high = (flat[:half], flat[half:])
        keep = jnp.where(upper, high, low)
        send = jnp.where(upper, low, high)
        flat = keep + exchange(send, axis, size)
    for (axis, size), upper in reversed(list(zip(steps, sides))):
        got = exchange(flat, axis, size)
        flat = jnp.where(upper, jnp.concatenate([got, flat]), jnp.concatenate([flat, got]))
    return flat.reshape(-1)[: x.size].reshape(shape)


def sum_steps():
    steps = []
    dp_count = lax.axis_size("dp")
    seq_count = lax.axis_size("seq")
    if dp_count & (dp_count - 1) or seq_count & (seq_count - 1):
        return None
    dp_bits = [1 << b for b in range(dp_count.bit_length() - 1)]
    seq_bits = [1 << b for b in range(seq_count.bit_length() - 1)]
    steps = [("dp", size) for size in dp_bits[:1]]
    steps += [("seq", size) for size in seq_bits]
    steps += [("dp", size) for size in dp_bits[1:]]
    return steps


def per_device(queries, keys, values, cotangent, taps, residue, skip, decay):
    rows = queries.shape[1]
    width = queries.shape[2]
    count = taps.shape[1]
    poles = decay.shape[0]
    q, k, v, c = queries[0], keys[0], values[0], cotangent[0]
    lead = jnp.stack([q[rows - RIM :], k[rows - RIM :], v[rows - RIM :]], 0)
    rim = passed_along(lead, "seq", 1)
    a = jnp.exp(-decay)
    f_bare, b_bare = run_states(q, k, v, c, jnp.zeros_like(lead), taps, a)
    with jax.named_scope("rim_share_of_states"):
        first = jnp.stack([q[:RIM], k[:RIM], v[:RIM]], 0).astype(F32)

        def head_feats(before):
            padded = jnp.concatenate([before, first], 1)
            return sum(taps[:, lag, None, :] * padded[:, RIM - lag : 2 * RIM - lag] for lag in range(count))

        with_rim = head_feats(rim.astype(F32))
        without = head_feats(jnp.zeros_like(first))
        d_product = with_rim[1] * with_rim[2] - without[1] * without[2]
        d_adjoint = c[:RIM].astype(F32) * (with_rim[0] - without[0])
        lags = jnp.arange(RIM, dtype=F32)
        f_local = f_bare + jnp.sum(
            jnp.exp(-decay[None] * (rows - 1 - lags)[:, None, None]) * d_product[:, None, :], 0
        )
        b_local = b_bare + jnp.sum(jnp.exp(-decay[None] * lags[:, None, None]) * d_adjoint[:, None, :], 0)
    with jax.named_scope("modal_state_scan"):
        s_in, g_in = scan_states(f_local, b_local, decay, rows, "seq")
    mixed, gq, gk, gv, tails, heads, grads = run_main(
        q, k, v, c, rim, taps, a, residue, skip.reshape(1, width), s_in, g_in
    )
    after = passed_along(heads, "seq", -1)
    ext = jnp.concatenate(
        [jnp.zeros((3, TAIL, width), F32), after[:, : count - 1], jnp.zeros((3, 1, width), F32)], 1
    )
    corr = sum(taps[:, lag, None, :] * ext[:, lag : lag + TAIL] for lag in range(count))
    fixed = (tails + corr).astype(jnp.bfloat16)
    streams = [
        lax.dynamic_update_slice(g, fixed[idx], (rows - TAIL, 0)) for idx, g in enumerate((gq, gk, gv))
    ]
    steps = sum_steps()
    if steps is None:
        totals = lax.psum(grads, ("seq", "dp"))
    else:
        with jax.named_scope("filter_grad_sum"):
            totals = butterfly_sum(grads, steps)
    grad_taps = totals[: 3 * count].reshape(3, count, width)
    grad_residue = totals[3 * count : 3 * count + poles]
    grad_skip = totals[3 * count + poles]
    return (
        mixed[None],
        streams[0][None],
        streams[1][None],
        streams[2][None],
        grad_taps,
        grad_residue,
        grad_skip,
    )


def solution(mesh):
    return jax.shard_map(
        per_device,
        mesh=mesh,
        in_specs=(
            P("dp", "seq", None),
            P("dp", "seq", None),
            P("dp", "seq", None),
            P("dp", "seq", None),
            P(),
            P(),
            P(),
            P(),
        ),
        out_specs=(
            P("dp", "seq", None),
            P("dp", "seq", None),
            P("dp", "seq", None),
            P("dp", "seq", None),
            P(),
            P(),
            P(),
        ),
        check_vma=False,
    )
```

```python
import functools

import jax
import jax.numpy as jnp
from jax import lax
from jax.experimental import pallas as pl
from jax.experimental.pallas import tpu as pltpu
from jax.sharding import PartitionSpec as P

LANES = 512
RIM = 8
TAIL = 16
BR = 16
F32 = jnp.float32


def passed_along(x, axis, by):
    count = lax.axis_size(axis)
    pairs = [(i, i + by) for i in range(count) if 0 <= i + by < count]
    return lax.ppermute(x, axis, pairs)


CHUNK = 256


def sublanes(lanes):
    return lax.broadcasted_iota(jnp.int32, (8, lanes), 0)


def feature_stream(pad_ref, taps_ref, s, out_ref, tiles=None):
    rows = out_ref.shape[1] if tiles is None else 8 * tiles
    count = taps_ref.shape[1]
    for c0 in range(0, out_ref.shape[2], CHUNK):
        cols = slice(c0, c0 + CHUNK)
        sub = sublanes(CHUNK)
        taps = [taps_ref[s, lag : lag + 1, cols] for lag in range(count)]
        prev = [pltpu.roll(pad_ref[s, 0:8, cols], lag, 0) for lag in range(1, count)]
        for i in range(rows // 8):
            cur = pad_ref[s, 8 * (i + 1) : 8 * (i + 2), cols]
            total = taps[0] * cur
            rolled = []
            for lag in range(1, count):
                turned = pltpu.roll(cur, lag, 0)
                total = total + taps[lag] * jnp.where(sub < lag, prev[lag - 1], turned)
                rolled.append(turned)
            prev = rolled
            out_ref[s, 8 * i : 8 * (i + 1), cols] = total


def fill_rows(x_refs, pad_ref, lo):
    for s, x_ref in enumerate(x_refs):
        pad_ref[s, RIM + lo : RIM + lo + BR, :] = x_ref[lo : lo + BR, :].astype(F32)


def states_kernel(
    q_ref, k_ref, v_ref, c_ref, rim_ref, taps_ref, a_ref, f_ref, b_ref, feat_ref, pad_ref, p_ref, z_ref
):
    rows = q_ref.shape[0]
    for s in range(3):
        pad_ref[s, 0:RIM, :] = rim_ref[s].astype(F32)
    for lo in range(0, rows, BR):
        fill_rows((q_ref, k_ref, v_ref), pad_ref, lo)
    for s in range(3):
        feature_stream(pad_ref, taps_ref, s, feat_ref)
    for lo in range(0, rows, BR):
        p_ref[lo : lo + BR, :] = feat_ref[1, lo : lo + BR, :] * feat_ref[2, lo : lo + BR, :]
        z_ref[lo : lo + BR, :] = c_ref[lo : lo + BR, :].astype(F32) * feat_ref[0, lo : lo + BR, :]
    a = a_ref[...]

    def step(i, carry):
        h, g = carry
        h = a * h + p_ref[pl.ds(i, 1), :]
        g = a * g + z_ref[pl.ds(rows - 1 - i, 1), :]
        return (h, g)

    zero = jnp.zeros_like(a)
    h, g = lax.fori_loop(0, rows, step, (zero, zero), unroll=8)
    f_ref[...] = h
    b_ref[...] = g


def fold(x):
    return x[0:8] + x[8:16]


def main_kernel(
    q_ref, k_ref, v_ref, c_ref, rim_ref, taps_ref, a_ref, r_ref, skip_ref, s_ref, g_ref, bare_ref,
    mixed_ref, gq_ref, gk_ref, gv_ref, tail_ref, head_ref, grads_ref,
    pad_ref, p_ref, z_ref, y_ref, u_ref, adj_ref, feat_ref,
):
    rows = q_ref.shape[0]
    count = taps_ref.shape[1]
    poles = a_ref.shape[0]
    lanes = q_ref.shape[1]
    for s in range(3):
        pad_ref[s, 0:RIM, :] = rim_ref[s].astype(F32)
    skip_sum = jnp.zeros((8, lanes), F32)
    for lo in range(0, rows, BR):
        fill_rows((q_ref, k_ref, v_ref), pad_ref, lo)
    for s in range(3):
        for lo in range(0, rows, BR):
            feat_ref[s, lo : lo + BR, :] = bare_ref[s, lo : lo + BR, :]
        feature_stream(pad_ref, taps_ref, s, feat_ref, tiles=1)
    for lo in range(0, rows, BR):
        fq = feat_ref[0, lo : lo + BR, :]
        fk = feat_ref[1, lo : lo + BR, :]
        fv = feat_ref[2, lo : lo + BR, :]
        p = fk * fv
        z = c_ref[lo : lo + BR, :].astype(F32) * fq
        p_ref[lo : lo + BR, :] = p
        z_ref[lo : lo + BR, :] = z
        skip_sum = skip_sum + fold(z * p)
    a = a_ref[...]
    r = r_ref[...]

    def step(i, carry):
        h, g, acc = carry
        h = a * h + p_ref[pl.ds(i, 1), :]
        acc = acc + z_ref[pl.ds(i, 1), :] * h
        y_ref[pl.ds(i, 1), :] = jnp.sum(r * h, axis=0, keepdims=True)
        back = rows - 1 - i
        g = a * g + z_ref[pl.ds(back, 1), :]
        u_ref[pl.ds(back, 1), :] = jnp.sum(r * g, axis=0, keepdims=True)
        return (h, g, acc)

    h, g, acc = lax.fori_loop(
        0, rows, step, (s_ref[...], g_ref[...], jnp.zeros_like(a)), unroll=8
    )
    skip = skip_ref[...]
    for lo in range(0, rows, BR):
        fq = feat_ref[0, lo : lo + BR, :]
        conv = y_ref[lo : lo + BR, :] + skip * p_ref[lo : lo + BR, :]
        mixed_ref[lo : lo + BR, :] = (fq * conv).astype(mixed_ref.dtype)
        adj_u = u_ref[lo : lo + BR, :] + skip * z_ref[lo : lo + BR, :]
        adj_ref[0, lo : lo + BR, :] = c_ref[lo : lo + BR, :].astype(F32) * conv
        adj_ref[1, lo : lo + BR, :] = adj_u * feat_ref[2, lo : lo + BR, :]
        adj_ref[2, lo : lo + BR, :] = adj_u * feat_ref[1, lo : lo + BR, :]
    zeros_rim = jnp.zeros((RIM, lanes), F32)
    outs = (gq_ref, gk_ref, gv_ref)
    for s in range(3):
        adj_ref[s, rows : rows + RIM, :] = zeros_rim
        head_ref[s] = adj_ref[s, 0:RIM, :]
    for s in range(3):
        for c0 in range(0, lanes, CHUNK):
            cols = slice(c0, c0 + CHUNK)
            sub = sublanes(CHUNK)
            taps = [taps_ref[s, lag : lag + 1, cols] for lag in range(count)]
            sums = [jnp.zeros((8, CHUNK), F32) for _ in range(count)]
            prev = [pltpu.roll(adj_ref[s, 0:8, cols], 8 - lag, 0) for lag in range(1, count)]
            done = []
            for i in range(rows // 8):
                cur = adj_ref[s, 8 * i : 8 * (i + 1), cols]
                after = adj_ref[s, 8 * (i + 1) : 8 * (i + 2), cols]
                x = pad_ref[s, RIM + 8 * i : RIM + 8 * (i + 1), cols]
                total = taps[0] * cur
                sums[0] = sums[0] + cur * x
                rolled = []
                for lag in range(1, count):
                    turned = pltpu.roll(after, 8 - lag, 0)
                    window = jnp.where(sub < 8 - lag, prev[lag - 1], turned)
                    total = total + taps[lag] * window
                    sums[lag] = sums[lag] + window * x
                    rolled.append(turned)
                prev = rolled
                done.append(total)
                if len(done) == 2:
                    both = jnp.concatenate(done, 0)
                    lo = 8 * (i - 1)
                    outs[s][lo : lo + BR, cols] = both.astype(outs[s].dtype)
                    if lo + BR == rows:
                        tail_ref[s, :, cols] = both[BR - TAIL :]
                    done = []
            for lag in range(count):
                value = jnp.sum(sums[lag], axis=0, keepdims=True)
                if lag > 0:
                    edge = adj_ref[s, 0:lag, cols] * pad_ref[s, RIM - lag : RIM, cols]
                    value = value + jnp.sum(edge, axis=0, keepdims=True)
                row = s * count + lag
                grads_ref[row : row + 1, cols] = value
    base = 3 * count
    grads_ref[base : base + poles, :] = acc
    grads_ref[base + poles : base + poles + 1, :] = jnp.sum(skip_sum, axis=0, keepdims=True)


def tile(shape, lanes):
    nd = len(shape)
    return pl.BlockSpec(tuple(shape[:-1]) + (lanes,), lambda i: (0,) * (nd - 1) + (i,))


def run_states(q, k, v, c, rim, taps, a):
    rows, width = q.shape
    poles = a.shape[0]
    lanes = min(LANES, width)
    ins = (q, k, v, c, rim, taps, a)
    return pl.pallas_call(
        states_kernel,
        grid=(width // lanes,),
        in_specs=[tile(x.shape, lanes) for x in ins],
        out_specs=[tile((poles, width), lanes), tile((poles, width), lanes), tile((3, rows, width), lanes)],
        out_shape=[jax.ShapeDtypeStruct((poles, width), F32)] * 2 + [jax.ShapeDtypeStruct((3, rows, width), F32)],
        scratch_shapes=[
            pltpu.VMEM((3, rows + RIM, lanes), F32),
            pltpu.VMEM((rows, lanes), F32),
            pltpu.VMEM((rows, lanes), F32),
        ],
    )(*ins)


def run_main(q, k, v, c, rim, taps, a, r, skip, s_in, g_in, bare):
    rows, width = q.shape
    poles = a.shape[0]
    count = taps.shape[1]
    lanes = min(LANES, width)
    ins = (q, k, v, c, rim, taps, a, r, skip, s_in, g_in, bare)
    out_shapes = [
        jax.ShapeDtypeStruct((rows, width), jnp.bfloat16),
        jax.ShapeDtypeStruct((rows, width), jnp.bfloat16),
        jax.ShapeDtypeStruct((rows, width), jnp.bfloat16),
        jax.ShapeDtypeStruct((rows, width), jnp.bfloat16),
        jax.ShapeDtypeStruct((3, TAIL, width), F32),
        jax.ShapeDtypeStruct((3, RIM, width), F32),
        jax.ShapeDtypeStruct((3 * count + poles + 1, width), F32),
    ]
    return pl.pallas_call(
        main_kernel,
        grid=(width // lanes,),
        in_specs=[tile(x.shape, lanes) for x in ins],
        out_specs=[tile(o.shape, lanes) for o in out_shapes],
        out_shape=out_shapes,
        scratch_shapes=[
            pltpu.VMEM((3, rows + RIM, lanes), F32),
            pltpu.VMEM((rows, lanes), F32),
            pltpu.VMEM((rows, lanes), F32),
            pltpu.VMEM((rows, lanes), F32),
            pltpu.VMEM((rows, lanes), F32),
            pltpu.VMEM((3, rows + RIM, lanes), F32),
            pltpu.VMEM((3, rows, lanes), F32),
        ],
    )(*ins)


def exchange(x, axis, size):
    count = lax.axis_size(axis)
    return lax.ppermute(x, axis, [(i, i ^ size) for i in range(count)])


def decayed(decay, rows, steps):
    return jnp.exp(-decay * (rows * steps).astype(F32))


def scan_four(final_f, final_b, decay, rows, axis, mine):
    jump = jnp.exp(-decay * float(rows))
    got = exchange(jnp.where(mine % 2 == 1, final_b, final_f), axis, 1)
    pair_f = final_f + jump * got
    pair_b = final_b + jump * got
    sent = jnp.where(mine == 1, pair_f, pair_b)
    across = lax.ppermute(sent, axis, [(1, 3), (2, 0)])
    diagonal = lax.ppermute(sent, axis, [(1, 2), (2, 1)])
    zero = jnp.zeros_like(final_f)
    incoming_f = jnp.where(
        mine == 3, got + jump * across, jnp.where(mine == 2, diagonal, jnp.where(mine == 1, got, zero))
    )
    incoming_b = jnp.where(
        mine == 0, got + jump * across, jnp.where(mine == 1, diagonal, jnp.where(mine == 2, got, zero))
    )
    return (incoming_f, incoming_b)


def scan_states(final_f, final_b, decay, rows, axis):
    count = lax.axis_size(axis)
    mine = lax.axis_index(axis)
    if count == 4:
        return scan_four(final_f, final_b, decay, rows, axis, mine)
    block_f, block_b = (final_f, final_b)
    incoming_f = jnp.zeros_like(final_f)
    incoming_b = jnp.zeros_like(final_b)
    levels = count.bit_length() - 1
    for level in range(levels):
        size = 1 << level
        upper = (mine // size) % 2 == 1
        pos = mine % size
        if level == levels - 1:
            sent = jnp.where(upper, block_b, block_f)
            half = sent.shape[1] // 2
            got = jnp.concatenate(
                [exchange(sent[:, :half], axis, size), exchange(sent[:, half:], axis, size)], 1
            )
            got_f, got_b = (got, got)
        else:
            got_f = exchange(block_f, axis, size)
            got_b = exchange(block_b, axis, size)
        incoming_f = incoming_f + jnp.where(upper, decayed(decay, rows, pos) * got_f, 0.0)
        incoming_b = incoming_b + jnp.where(upper, 0.0, decayed(decay, rows, size - 1 - pos) * got_b)
        if level < levels - 1:
            jump = jnp.exp(-decay * float(rows * size))
            block_f = jnp.where(upper, block_f + jump * got_f, got_f + jump * block_f)
            block_b = jnp.where(upper, got_b + jump * block_b, block_b + jump * got_b)
    return (incoming_f, incoming_b)


def butterfly_sum(x, steps):
    shape = x.shape
    flat = x.reshape(-1)
    pieces = 1 << len(steps)
    unit = pieces * 128
    padded = -(-flat.shape[0] // unit) * unit
    flat = jnp.pad(flat, (0, padded - flat.shape[0])).reshape(-1, 128)
    sides = []
    for axis, size in steps:
        upper = (lax.axis_index(axis) // size) % 2 == 1
        sides.append(upper)
        half = flat.shape[0] // 2
        low, high = (flat[:half], flat[half:])
        keep = jnp.where(upper, high, low)
        send = jnp.where(upper, low, high)
        flat = keep + exchange(send, axis, size)
    for (axis, size), upper in reversed(list(zip(steps, sides))):
        got = exchange(flat, axis, size)
        flat = jnp.where(upper, jnp.concatenate([got, flat]), jnp.concatenate([flat, got]))
    return flat.reshape(-1)[: x.size].reshape(shape)


def sum_steps():
    steps = []
    dp_count = lax.axis_size("dp")
    seq_count = lax.axis_size("seq")
    if dp_count & (dp_count - 1) or seq_count & (seq_count - 1):
        return None
    dp_bits = [1 << b for b in range(dp_count.bit_length() - 1)]
    seq_bits = [1 << b for b in range(seq_count.bit_length() - 1)]
    steps = [("dp", size) for size in dp_bits[:1]]
    steps += [("seq", size) for size in seq_bits]
    steps += [("dp", size) for size in dp_bits[1:]]
    return steps


def per_device(queries, keys, values, cotangent, taps, residue, skip, decay):
    rows = queries.shape[1]
    width = queries.shape[2]
    count = taps.shape[1]
    poles = decay.shape[0]
    q, k, v, c = queries[0], keys[0], values[0], cotangent[0]
    lead = jnp.stack([q[rows - RIM :], k[rows - RIM :], v[rows - RIM :]], 0)
    rim = passed_along(lead, "seq", 1)
    a = jnp.exp(-decay)
    f_bare, b_bare, bare_feats = run_states(q, k, v, c, jnp.zeros_like(lead), taps, a)
    with jax.named_scope("rim_share_of_states"):
        first = jnp.stack([q[:RIM], k[:RIM], v[:RIM]], 0).astype(F32)

        def head_feats(before):
            padded = jnp.concatenate([before, first], 1)
            return sum(taps[:, lag, None, :] * padded[:, RIM - lag : 2 * RIM - lag] for lag in range(count))

        with_rim = head_feats(rim.astype(F32))
        without = head_feats(jnp.zeros_like(first))
        d_product = with_rim[1] * with_rim[2] - without[1] * without[2]
        d_adjoint = c[:RIM].astype(F32) * (with_rim[0] - without[0])
        lags = jnp.arange(RIM, dtype=F32)
        f_local = f_bare + jnp.sum(
            jnp.exp(-decay[None] * (rows - 1 - lags)[:, None, None]) * d_product[:, None, :], 0
        )
        b_local = b_bare + jnp.sum(jnp.exp(-decay[None] * lags[:, None, None]) * d_adjoint[:, None, :], 0)
    with jax.named_scope("modal_state_scan"):
        s_in, g_in = scan_states(f_local, b_local, decay, rows, "seq")
    mixed, gq, gk, gv, tails, heads, grads = run_main(
        q, k, v, c, rim, taps, a, residue, skip.reshape(1, width), s_in, g_in, bare_feats
    )
    after = passed_along(heads, "seq", -1)
    ext = jnp.concatenate(
        [jnp.zeros((3, TAIL, width), F32), after[:, : count - 1], jnp.zeros((3, 1, width), F32)], 1
    )
    corr = sum(taps[:, lag, None, :] * ext[:, lag : lag + TAIL] for lag in range(count))
    fixed = (tails + corr).astype(jnp.bfloat16)
    streams = [
        lax.dynamic_update_slice(g, fixed[idx], (rows - TAIL, 0)) for idx, g in enumerate((gq, gk, gv))
    ]
    steps = sum_steps()
    if steps is None:
        totals = lax.psum(grads, ("seq", "dp"))
    else:
        with jax.named_scope("filter_grad_sum"):
            totals = butterfly_sum(grads, steps)
    grad_taps = totals[: 3 * count].reshape(3, count, width)
    grad_residue = totals[3 * count : 3 * count + poles]
    grad_skip = totals[3 * count + poles]
    return (
        mixed[None],
        streams[0][None],
        streams[1][None],
        streams[2][None],
        grad_taps,
        grad_residue,
        grad_skip,
    )


def solution(mesh):
    return jax.shard_map(
        per_device,
        mesh=mesh,
        in_specs=(
            P("dp", "seq", None),
            P("dp", "seq", None),
            P("dp", "seq", None),
            P("dp", "seq", None),
            P(),
            P(),
            P(),
            P(),
        ),
        out_specs=(
            P("dp", "seq", None),
            P("dp", "seq", None),
            P("dp", "seq", None),
            P("dp", "seq", None),
            P(),
            P(),
            P(),
        ),
        check_vma=False,
    )
```

```python
import functools

import jax
import jax.numpy as jnp
from jax import lax
from jax.experimental import pallas as pl
from jax.experimental.pallas import tpu as pltpu
from jax.sharding import PartitionSpec as P

LANES = 512
RIM = 8
TAIL = 16
BR = 16
F32 = jnp.float32


def passed_along(x, axis, by):
    count = lax.axis_size(axis)
    pairs = [(i, i + by) for i in range(count) if 0 <= i + by < count]
    return lax.ppermute(x, axis, pairs)


CHUNK = 256


def sublanes(lanes):
    return lax.broadcasted_iota(jnp.int32, (8, lanes), 0)


def feature_stream(pad_ref, taps_ref, s, out_ref, tiles=None):
    rows = out_ref.shape[1] if tiles is None else 8 * tiles
    count = taps_ref.shape[1]
    for c0 in range(0, out_ref.shape[2], CHUNK):
        cols = slice(c0, c0 + CHUNK)
        sub = sublanes(CHUNK)
        taps = [taps_ref[s, lag : lag + 1, cols] for lag in range(count)]
        prev = [pltpu.roll(pad_ref[s, 0:8, cols], lag, 0) for lag in range(1, count)]
        for i in range(rows // 8):
            cur = pad_ref[s, 8 * (i + 1) : 8 * (i + 2), cols]
            total = taps[0] * cur
            rolled = []
            for lag in range(1, count):
                turned = pltpu.roll(cur, lag, 0)
                total = total + taps[lag] * jnp.where(sub < lag, prev[lag - 1], turned)
                rolled.append(turned)
            prev = rolled
            out_ref[s, 8 * i : 8 * (i + 1), cols] = total


def fill_rows(x_refs, pad_ref, lo):
    for s, x_ref in enumerate(x_refs):
        pad_ref[s, RIM + lo : RIM + lo + BR, :] = x_ref[lo : lo + BR, :].astype(F32)


def states_kernel(
    q_ref, k_ref, v_ref, c_ref, rim_ref, taps_ref, a_ref, f_ref, b_ref, feat_ref, pad_ref, p_ref, z_ref
):
    rows = q_ref.shape[0]
    for s in range(3):
        pad_ref[s, 0:RIM, :] = rim_ref[s].astype(F32)
    for lo in range(0, rows, BR):
        fill_rows((q_ref, k_ref, v_ref), pad_ref, lo)
    for s in range(3):
        feature_stream(pad_ref, taps_ref, s, feat_ref)
    for lo in range(0, rows, BR):
        p_ref[lo : lo + BR, :] = feat_ref[1, lo : lo + BR, :] * feat_ref[2, lo : lo + BR, :]
        z_ref[lo : lo + BR, :] = c_ref[lo : lo + BR, :].astype(F32) * feat_ref[0, lo : lo + BR, :]
    a = a_ref[...]

    def step(i, carry):
        h, g = carry
        h = a * h + p_ref[pl.ds(i, 1), :]
        g = a * g + z_ref[pl.ds(rows - 1 - i, 1), :]
        return (h, g)

    zero = jnp.zeros_like(a)
    h, g = lax.fori_loop(0, rows, step, (zero, zero), unroll=8)
    f_ref[...] = h
    b_ref[...] = g


def fold(x):
    return x[0:8] + x[8:16]


def main_kernel(
    q_ref, k_ref, v_ref, c_ref, rim_ref, taps_ref, a_ref, r_ref, skip_ref, s_ref, g_ref, bare_ref,
    mixed_ref, gq_ref, gk_ref, gv_ref, tail_ref, head_ref, grads_ref,
    pad_ref, p_ref, z_ref, y_ref, u_ref, adj_ref, feat_ref,
):
    rows = q_ref.shape[0]
    count = taps_ref.shape[1]
    poles = a_ref.shape[0]
    lanes = q_ref.shape[1]
    for s in range(3):
        pad_ref[s, 0:RIM, :] = rim_ref[s].astype(F32)
    skip_sum = jnp.zeros((8, lanes), F32)
    for lo in range(0, rows, BR):
        fill_rows((q_ref, k_ref, v_ref), pad_ref, lo)
    for s in range(3):
        for lo in range(0, rows, BR):
            feat_ref[s, lo : lo + BR, :] = bare_ref[s, lo : lo + BR, :]
        feature_stream(pad_ref, taps_ref, s, feat_ref, tiles=1)
    for lo in range(0, rows, BR):
        fq = feat_ref[0, lo : lo + BR, :]
        fk = feat_ref[1, lo : lo + BR, :]
        fv = feat_ref[2, lo : lo + BR, :]
        p = fk * fv
        z = c_ref[lo : lo + BR, :].astype(F32) * fq
        p_ref[lo : lo + BR, :] = p
        z_ref[lo : lo + BR, :] = z
        skip_sum = skip_sum + fold(z * p)
    a = a_ref[...]
    r = r_ref[...]

    def step(i, carry):
        h, g, acc = carry
        h = a * h + p_ref[pl.ds(i, 1), :]
        acc = acc + z_ref[pl.ds(i, 1), :] * h
        y_ref[pl.ds(i, 1), :] = jnp.sum(r * h, axis=0, keepdims=True)
        back = rows - 1 - i
        g = a * g + z_ref[pl.ds(back, 1), :]
        u_ref[pl.ds(back, 1), :] = jnp.sum(r * g, axis=0, keepdims=True)
        return (h, g, acc)

    h, g, acc = lax.fori_loop(
        0, rows, step, (s_ref[...], g_ref[...], jnp.zeros_like(a)), unroll=8
    )
    skip = skip_ref[...]
    for lo in range(0, rows, BR):
        fq = feat_ref[0, lo : lo + BR, :]
        conv = y_ref[lo : lo + BR, :] + skip * p_ref[lo : lo + BR, :]
        mixed_ref[lo : lo + BR, :] = (fq * conv).astype(mixed_ref.dtype)
        adj_u = u_ref[lo : lo + BR, :] + skip * z_ref[lo : lo + BR, :]
        adj_ref[0, lo : lo + BR, :] = c_ref[lo : lo + BR, :].astype(F32) * conv
        adj_ref[1, lo : lo + BR, :] = adj_u * feat_ref[2, lo : lo + BR, :]
        adj_ref[2, lo : lo + BR, :] = adj_u * feat_ref[1, lo : lo + BR, :]
    zeros_rim = jnp.zeros((RIM, lanes), F32)
    outs = (gq_ref, gk_ref, gv_ref)
    for s in range(3):
        adj_ref[s, rows : rows + RIM, :] = zeros_rim
        head_ref[s] = adj_ref[s, 0:RIM, :]
    for s in range(3):
        for c0 in range(0, lanes, CHUNK):
            cols = slice(c0, c0 + CHUNK)
            sub = sublanes(CHUNK)
            taps = [taps_ref[s, lag : lag + 1, cols] for lag in range(count)]
            sums = [jnp.zeros((8, CHUNK), F32) for _ in range(count)]
            prev = [pltpu.roll(adj_ref[s, 0:8, cols], 8 - lag, 0) for lag in range(1, count)]
            done = []
            for i in range(rows // 8):
                cur = adj_ref[s, 8 * i : 8 * (i + 1), cols]
                after = adj_ref[s, 8 * (i + 1) : 8 * (i + 2), cols]
                x = pad_ref[s, RIM + 8 * i : RIM + 8 * (i + 1), cols]
                total = taps[0] * cur
                sums[0] = sums[0] + cur * x
                rolled = []
                for lag in range(1, count):
                    turned = pltpu.roll(after, 8 - lag, 0)
                    window = jnp.where(sub < 8 - lag, prev[lag - 1], turned)
                    total = total + taps[lag] * window
                    sums[lag] = sums[lag] + window * x
                    rolled.append(turned)
                prev = rolled
                done.append(total)
                if len(done) == 2:
                    both = jnp.concatenate(done, 0)
                    lo = 8 * (i - 1)
                    outs[s][lo : lo + BR, cols] = both.astype(outs[s].dtype)
                    if lo + BR == rows:
                        tail_ref[s, :, cols] = both[BR - TAIL :]
                    done = []
            for lag in range(count):
                value = jnp.sum(sums[lag], axis=0, keepdims=True)
                if lag > 0:
                    edge = adj_ref[s, 0:lag, cols] * pad_ref[s, RIM - lag : RIM, cols]
                    value = value + jnp.sum(edge, axis=0, keepdims=True)
                row = s * count + lag
                grads_ref[row : row + 1, cols] = value
    base = 3 * count
    grads_ref[base : base + poles, :] = acc
    grads_ref[base + poles : base + poles + 1, :] = jnp.sum(skip_sum, axis=0, keepdims=True)


def tile(shape, lanes):
    nd = len(shape)
    return pl.BlockSpec(tuple(shape[:-1]) + (lanes,), lambda i: (0,) * (nd - 1) + (i,))


def run_states(q, k, v, c, rim, taps, a):
    rows, width = q.shape
    poles = a.shape[0]
    lanes = min(LANES, width)
    ins = (q, k, v, c, rim, taps, a)
    return pl.pallas_call(
        states_kernel,
        grid=(width // lanes,),
        in_specs=[tile(x.shape, lanes) for x in ins],
        out_specs=[tile((poles, width), lanes), tile((poles, width), lanes), tile((3, rows, width), lanes)],
        out_shape=[jax.ShapeDtypeStruct((poles, width), F32)] * 2 + [jax.ShapeDtypeStruct((3, rows, width), F32)],
        scratch_shapes=[
            pltpu.VMEM((3, rows + RIM, lanes), F32),
            pltpu.VMEM((rows, lanes), F32),
            pltpu.VMEM((rows, lanes), F32),
        ],
    )(*ins)


def run_main(q, k, v, c, rim, taps, a, r, skip, s_in, g_in, bare):
    rows, width = q.shape
    poles = a.shape[0]
    count = taps.shape[1]
    lanes = min(LANES, width)
    ins = (q, k, v, c, rim, taps, a, r, skip, s_in, g_in, bare)
    out_shapes = [
        jax.ShapeDtypeStruct((rows, width), jnp.bfloat16),
        jax.ShapeDtypeStruct((rows, width), jnp.bfloat16),
        jax.ShapeDtypeStruct((rows, width), jnp.bfloat16),
        jax.ShapeDtypeStruct((rows, width), jnp.bfloat16),
        jax.ShapeDtypeStruct((3, TAIL, width), F32),
        jax.ShapeDtypeStruct((3, RIM, width), F32),
        jax.ShapeDtypeStruct((3 * count + poles + 1, width), F32),
    ]
    return pl.pallas_call(
        main_kernel,
        grid=(width // lanes,),
        in_specs=[tile(x.shape, lanes) for x in ins],
        out_specs=[tile(o.shape, lanes) for o in out_shapes],
        out_shape=out_shapes,
        scratch_shapes=[
            pltpu.VMEM((3, rows + RIM, lanes), F32),
            pltpu.VMEM((rows, lanes), F32),
            pltpu.VMEM((rows, lanes), F32),
            pltpu.VMEM((rows, lanes), F32),
            pltpu.VMEM((rows, lanes), F32),
            pltpu.VMEM((3, rows + RIM, lanes), F32),
            pltpu.VMEM((3, rows, lanes), F32),
        ],
    )(*ins)


def exchange(x, axis, size):
    count = lax.axis_size(axis)
    return lax.ppermute(x, axis, [(i, i ^ size) for i in range(count)])


def decayed(decay, rows, steps):
    return jnp.exp(-decay * (rows * steps).astype(F32))


def scan_four(final_f, final_b, decay, rows, axis, mine):
    jump = jnp.exp(-decay * float(rows))
    got = exchange(jnp.where(mine % 2 == 1, final_b, final_f), axis, 1)
    pair_f = final_f + jump * got
    pair_b = final_b + jump * got
    sent = jnp.where(mine == 1, pair_f, pair_b)
    across = lax.ppermute(sent, axis, [(1, 3), (2, 0)])
    diagonal = lax.ppermute(sent, axis, [(1, 2), (2, 1)])
    zero = jnp.zeros_like(final_f)
    incoming_f = jnp.where(
        mine == 3, got + jump * across, jnp.where(mine == 2, diagonal, jnp.where(mine == 1, got, zero))
    )
    incoming_b = jnp.where(
        mine == 0, got + jump * across, jnp.where(mine == 1, diagonal, jnp.where(mine == 2, got, zero))
    )
    return (incoming_f, incoming_b)


def scan_states(final_f, final_b, decay, rows, axis):
    count = lax.axis_size(axis)
    mine = lax.axis_index(axis)
    if count == 4:
        return scan_four(final_f, final_b, decay, rows, axis, mine)
    block_f, block_b = (final_f, final_b)
    incoming_f = jnp.zeros_like(final_f)
    incoming_b = jnp.zeros_like(final_b)
    levels = count.bit_length() - 1
    for level in range(levels):
        size = 1 << level
        upper = (mine // size) % 2 == 1
        pos = mine % size
        if level == levels - 1:
            sent = jnp.where(upper, block_b, block_f)
            half = sent.shape[1] // 2
            got = jnp.concatenate(
                [exchange(sent[:, :half], axis, size), exchange(sent[:, half:], axis, size)], 1
            )
            got_f, got_b = (got, got)
        else:
            got_f = exchange(block_f, axis, size)
            got_b = exchange(block_b, axis, size)
        incoming_f = incoming_f + jnp.where(upper, decayed(decay, rows, pos) * got_f, 0.0)
        incoming_b = incoming_b + jnp.where(upper, 0.0, decayed(decay, rows, size - 1 - pos) * got_b)
        if level < levels - 1:
            jump = jnp.exp(-decay * float(rows * size))
            block_f = jnp.where(upper, block_f + jump * got_f, got_f + jump * block_f)
            block_b = jnp.where(upper, got_b + jump * block_b, block_b + jump * got_b)
    return (incoming_f, incoming_b)


def butterfly_sum(x, steps):
    shape = x.shape
    flat = x.reshape(-1)
    pieces = 1 << len(steps)
    unit = pieces * 128
    padded = -(-flat.shape[0] // unit) * unit
    flat = jnp.pad(flat, (0, padded - flat.shape[0])).reshape(-1, 128)
    sides = []
    for axis, size in steps:
        upper = (lax.axis_index(axis) // size) % 2 == 1
        sides.append(upper)
        half = flat.shape[0] // 2
        low, high = (flat[:half], flat[half:])
        keep = jnp.where(upper, high, low)
        send = jnp.where(upper, low, high)
        flat = keep + exchange(send, axis, size)
    for (axis, size), upper in reversed(list(zip(steps, sides))):
        got = exchange(flat, axis, size)
        flat = jnp.where(upper, jnp.concatenate([got, flat]), jnp.concatenate([flat, got]))
    return flat.reshape(-1)[: x.size].reshape(shape)


def sum_steps():
    steps = []
    dp_count = lax.axis_size("dp")
    seq_count = lax.axis_size("seq")
    if dp_count & (dp_count - 1) or seq_count & (seq_count - 1):
        return None
    dp_bits = [1 << b for b in range(dp_count.bit_length() - 1)]
    seq_bits = [1 << b for b in range(seq_count.bit_length() - 1)]
    steps = [("dp", size) for size in dp_bits[:1]]
    steps += [("seq", size) for size in seq_bits]
    steps += [("dp", size) for size in dp_bits[1:]]
    return steps


def per_device(queries, keys, values, cotangent, taps, residue, skip, decay):
    rows = queries.shape[1]
    width = queries.shape[2]
    count = taps.shape[1]
    poles = decay.shape[0]
    q, k, v, c = queries[0], keys[0], values[0], cotangent[0]
    lead = jnp.stack([q[rows - RIM :], k[rows - RIM :], v[rows - RIM :]], 0)
    rim = passed_along(lead, "seq", 1)
    a = jnp.exp(-decay)
    f_bare, b_bare, bare_feats = run_states(q, k, v, c, jnp.zeros_like(lead), taps, a)
    with jax.named_scope("rim_share_of_states"):
        first = jnp.stack([q[:RIM], k[:RIM], v[:RIM]], 0).astype(F32)

        def head_feats(before):
            padded = jnp.concatenate([before, first], 1)
            return sum(taps[:, lag, None, :] * padded[:, RIM - lag : 2 * RIM - lag] for lag in range(count))

        with_rim = head_feats(rim.astype(F32))
        without = head_feats(jnp.zeros_like(first))
        d_product = with_rim[1] * with_rim[2] - without[1] * without[2]
        d_adjoint = c[:RIM].astype(F32) * (with_rim[0] - without[0])
        powers = [jnp.ones_like(a)]
        for _ in range(RIM - 1):
            powers.append(powers[-1] * a)
        far = jnp.exp(-decay * float(rows - RIM))
        f_local = f_bare + sum(far * powers[RIM - 1 - t] * d_product[t] for t in range(RIM))
        b_local = b_bare + sum(powers[t] * d_adjoint[t] for t in range(RIM))
    with jax.named_scope("modal_state_scan"):
        s_in, g_in = scan_states(f_local, b_local, decay, rows, "seq")
    mixed, gq, gk, gv, tails, heads, grads = run_main(
        q, k, v, c, rim, taps, a, residue, skip.reshape(1, width), s_in, g_in, bare_feats
    )
    after = passed_along(heads, "seq", -1)
    ext = jnp.concatenate(
        [jnp.zeros((3, TAIL, width), F32), after[:, : count - 1], jnp.zeros((3, 1, width), F32)], 1
    )
    corr = sum(taps[:, lag, None, :] * ext[:, lag : lag + TAIL] for lag in range(count))
    fixed = (tails + corr).astype(jnp.bfloat16)
    streams = [
        lax.dynamic_update_slice(g, fixed[idx], (rows - TAIL, 0)) for idx, g in enumerate((gq, gk, gv))
    ]
    steps = sum_steps()
    if steps is None:
        totals = lax.psum(grads, ("seq", "dp"))
    else:
        with jax.named_scope("filter_grad_sum"):
            totals = butterfly_sum(grads, steps)
    grad_taps = totals[: 3 * count].reshape(3, count, width)
    grad_residue = totals[3 * count : 3 * count + poles]
    grad_skip = totals[3 * count + poles]
    return (
        mixed[None],
        streams[0][None],
        streams[1][None],
        streams[2][None],
        grad_taps,
        grad_residue,
        grad_skip,
    )


def solution(mesh):
    return jax.shard_map(
        per_device,
        mesh=mesh,
        in_specs=(
            P("dp", "seq", None),
            P("dp", "seq", None),
            P("dp", "seq", None),
            P("dp", "seq", None),
            P(),
            P(),
            P(),
            P(),
        ),
        out_specs=(
            P("dp", "seq", None),
            P("dp", "seq", None),
            P("dp", "seq", None),
            P("dp", "seq", None),
            P(),
            P(),
            P(),
        ),
        check_vma=False,
    )
```

```python
import functools

import jax
import jax.numpy as jnp
from jax import lax
from jax.experimental import pallas as pl
from jax.experimental.pallas import tpu as pltpu
from jax.sharding import PartitionSpec as P

LANES = 512
RIM = 8
TAIL = 16
BR = 16
F32 = jnp.float32


def passed_along(x, axis, by):
    count = lax.axis_size(axis)
    pairs = [(i, i + by) for i in range(count) if 0 <= i + by < count]
    return lax.ppermute(x, axis, pairs)


CHUNK = 256


def sublanes(lanes):
    return lax.broadcasted_iota(jnp.int32, (8, lanes), 0)


def feature_stream(pad_ref, taps_ref, s, out_ref, tiles=None):
    rows = out_ref.shape[1] if tiles is None else 8 * tiles
    count = taps_ref.shape[1]
    for c0 in range(0, out_ref.shape[2], CHUNK):
        cols = slice(c0, c0 + CHUNK)
        sub = sublanes(CHUNK)
        taps = [taps_ref[s, lag : lag + 1, cols] for lag in range(count)]
        prev = [pltpu.roll(pad_ref[s, 0:8, cols], lag, 0) for lag in range(1, count)]
        for i in range(rows // 8):
            cur = pad_ref[s, 8 * (i + 1) : 8 * (i + 2), cols]
            total = taps[0] * cur
            rolled = []
            for lag in range(1, count):
                turned = pltpu.roll(cur, lag, 0)
                total = total + taps[lag] * jnp.where(sub < lag, prev[lag - 1], turned)
                rolled.append(turned)
            prev = rolled
            out_ref[s, 8 * i : 8 * (i + 1), cols] = total


def fill_rows(x_refs, pad_ref, lo):
    for s, x_ref in enumerate(x_refs):
        pad_ref[s, RIM + lo : RIM + lo + BR, :] = x_ref[lo : lo + BR, :].astype(F32)


def states_kernel(
    q_ref, k_ref, v_ref, c_ref, rim_ref, taps_ref, a_ref, f_ref, b_ref, feat_ref, pad_ref, p_ref, z_ref
):
    rows = q_ref.shape[0]
    for s in range(3):
        pad_ref[s, 0:RIM, :] = rim_ref[s].astype(F32)
    for lo in range(0, rows, BR):
        fill_rows((q_ref, k_ref, v_ref), pad_ref, lo)
    for s in range(3):
        feature_stream(pad_ref, taps_ref, s, feat_ref)
    for lo in range(0, rows, BR):
        p_ref[lo : lo + BR, :] = feat_ref[1, lo : lo + BR, :] * feat_ref[2, lo : lo + BR, :]
        z_ref[lo : lo + BR, :] = c_ref[lo : lo + BR, :].astype(F32) * feat_ref[0, lo : lo + BR, :]
    a = a_ref[...]

    def step(i, carry):
        h, g = carry
        h = a * h + p_ref[pl.ds(i, 1), :]
        g = a * g + z_ref[pl.ds(rows - 1 - i, 1), :]
        return (h, g)

    zero = jnp.zeros_like(a)
    h, g = lax.fori_loop(0, rows, step, (zero, zero), unroll=8)
    f_ref[...] = h
    b_ref[...] = g


def fold(x):
    return x[0:8] + x[8:16]


def main_kernel(
    q_ref, k_ref, v_ref, c_ref, rim_ref, taps_ref, a_ref, r_ref, skip_ref, s_ref, g_ref, bare_ref,
    mixed_ref, gq_ref, gk_ref, gv_ref, tail_ref, head_ref, grads_ref,
    pad_ref, p_ref, z_ref, y_ref, u_ref, adj_ref, feat_ref,
):
    rows = q_ref.shape[0]
    count = taps_ref.shape[1]
    poles = a_ref.shape[0]
    lanes = q_ref.shape[1]
    for s in range(3):
        pad_ref[s, 0:RIM, :] = rim_ref[s].astype(F32)
    skip_sum = jnp.zeros((8, lanes), F32)
    for lo in range(0, rows, BR):
        fill_rows((q_ref, k_ref, v_ref), pad_ref, lo)
    for s in range(3):
        for lo in range(0, rows, BR):
            feat_ref[s, lo : lo + BR, :] = bare_ref[s, lo : lo + BR, :]
        feature_stream(pad_ref, taps_ref, s, feat_ref, tiles=1)
    for lo in range(0, rows, BR):
        fq = feat_ref[0, lo : lo + BR, :]
        fk = feat_ref[1, lo : lo + BR, :]
        fv = feat_ref[2, lo : lo + BR, :]
        p = fk * fv
        z = c_ref[lo : lo + BR, :].astype(F32) * fq
        p_ref[lo : lo + BR, :] = p
        z_ref[lo : lo + BR, :] = z
        skip_sum = skip_sum + fold(z * p)
    a = a_ref[...]
    r = r_ref[...]

    def step(i, carry):
        h, g, acc = carry
        h = a * h + p_ref[pl.ds(i, 1), :]
        acc = acc + z_ref[pl.ds(i, 1), :] * h
        y_ref[pl.ds(i, 1), :] = jnp.sum(r * h, axis=0, keepdims=True)
        back = rows - 1 - i
        g = a * g + z_ref[pl.ds(back, 1), :]
        u_ref[pl.ds(back, 1), :] = jnp.sum(r * g, axis=0, keepdims=True)
        return (h, g, acc)

    h, g, acc = lax.fori_loop(
        0, rows, step, (s_ref[...], g_ref[...], jnp.zeros_like(a)), unroll=8
    )
    skip = skip_ref[...]
    for lo in range(0, rows, BR):
        fq = feat_ref[0, lo : lo + BR, :]
        conv = y_ref[lo : lo + BR, :] + skip * p_ref[lo : lo + BR, :]
        mixed_ref[lo : lo + BR, :] = (fq * conv).astype(mixed_ref.dtype)
        adj_u = u_ref[lo : lo + BR, :] + skip * z_ref[lo : lo + BR, :]
        adj_ref[0, lo : lo + BR, :] = c_ref[lo : lo + BR, :].astype(F32) * conv
        adj_ref[1, lo : lo + BR, :] = adj_u * feat_ref[2, lo : lo + BR, :]
        adj_ref[2, lo : lo + BR, :] = adj_u * feat_ref[1, lo : lo + BR, :]
    zeros_rim = jnp.zeros((RIM, lanes), F32)
    outs = (gq_ref, gk_ref, gv_ref)
    for s in range(3):
        adj_ref[s, rows : rows + RIM, :] = zeros_rim
        head_ref[s] = adj_ref[s, 0:RIM, :]
    for s in range(3):
        for c0 in range(0, lanes, CHUNK):
            cols = slice(c0, c0 + CHUNK)
            sub = sublanes(CHUNK)
            taps = [taps_ref[s, lag : lag + 1, cols] for lag in range(count)]
            sums = [jnp.zeros((8, CHUNK), F32) for _ in range(count)]
            prev = [pltpu.roll(adj_ref[s, 0:8, cols], 8 - lag, 0) for lag in range(1, count)]
            done = []
            for i in range(rows // 8):
                cur = adj_ref[s, 8 * i : 8 * (i + 1), cols]
                after = adj_ref[s, 8 * (i + 1) : 8 * (i + 2), cols]
                x = pad_ref[s, RIM + 8 * i : RIM + 8 * (i + 1), cols]
                total = taps[0] * cur
                sums[0] = sums[0] + cur * x
                rolled = []
                for lag in range(1, count):
                    turned = pltpu.roll(after, 8 - lag, 0)
                    window = jnp.where(sub < 8 - lag, prev[lag - 1], turned)
                    total = total + taps[lag] * window
                    sums[lag] = sums[lag] + window * x
                    rolled.append(turned)
                prev = rolled
                done.append(total)
                if len(done) == 2:
                    both = jnp.concatenate(done, 0)
                    lo = 8 * (i - 1)
                    outs[s][lo : lo + BR, cols] = both.astype(outs[s].dtype)
                    if lo + BR == rows:
                        tail_ref[s, :, cols] = both[BR - TAIL :]
                    done = []
            for lag in range(count):
                value = jnp.sum(sums[lag], axis=0, keepdims=True)
                if lag > 0:
                    edge = adj_ref[s, 0:lag, cols] * pad_ref[s, RIM - lag : RIM, cols]
                    value = value + jnp.sum(edge, axis=0, keepdims=True)
                row = s * count + lag
                grads_ref[row : row + 1, cols] = value
    base = 3 * count
    grads_ref[base : base + poles, :] = acc
    grads_ref[base + poles : base + poles + 1, :] = jnp.sum(skip_sum, axis=0, keepdims=True)


def tile(shape, lanes):
    nd = len(shape)
    return pl.BlockSpec(tuple(shape[:-1]) + (lanes,), lambda i: (0,) * (nd - 1) + (i,))


def run_states(q, k, v, c, rim, taps, a):
    rows, width = q.shape
    poles = a.shape[0]
    lanes = min(LANES, width)
    ins = (q, k, v, c, rim, taps, a)
    return pl.pallas_call(
        states_kernel,
        grid=(width // lanes,),
        in_specs=[tile(x.shape, lanes) for x in ins],
        out_specs=[tile((poles, width), lanes), tile((poles, width), lanes), tile((3, rows, width), lanes)],
        out_shape=[jax.ShapeDtypeStruct((poles, width), F32)] * 2 + [jax.ShapeDtypeStruct((3, rows, width), F32)],
        scratch_shapes=[
            pltpu.VMEM((3, rows + RIM, lanes), F32),
            pltpu.VMEM((rows, lanes), F32),
            pltpu.VMEM((rows, lanes), F32),
        ],
    )(*ins)


def run_main(q, k, v, c, rim, taps, a, r, skip, s_in, g_in, bare):
    rows, width = q.shape
    poles = a.shape[0]
    count = taps.shape[1]
    lanes = min(LANES // 2, width)
    ins = (q, k, v, c, rim, taps, a, r, skip, s_in, g_in, bare)
    out_shapes = [
        jax.ShapeDtypeStruct((rows, width), jnp.bfloat16),
        jax.ShapeDtypeStruct((rows, width), jnp.bfloat16),
        jax.ShapeDtypeStruct((rows, width), jnp.bfloat16),
        jax.ShapeDtypeStruct((rows, width), jnp.bfloat16),
        jax.ShapeDtypeStruct((3, TAIL, width), F32),
        jax.ShapeDtypeStruct((3, RIM, width), F32),
        jax.ShapeDtypeStruct((3 * count + poles + 1, width), F32),
    ]
    return pl.pallas_call(
        main_kernel,
        grid=(width // lanes,),
        in_specs=[tile(x.shape, lanes) for x in ins],
        out_specs=[tile(o.shape, lanes) for o in out_shapes],
        out_shape=out_shapes,
        scratch_shapes=[
            pltpu.VMEM((3, rows + RIM, lanes), F32),
            pltpu.VMEM((rows, lanes), F32),
            pltpu.VMEM((rows, lanes), F32),
            pltpu.VMEM((rows, lanes), F32),
            pltpu.VMEM((rows, lanes), F32),
            pltpu.VMEM((3, rows + RIM, lanes), F32),
            pltpu.VMEM((3, rows, lanes), F32),
        ],
    )(*ins)


def exchange(x, axis, size):
    count = lax.axis_size(axis)
    return lax.ppermute(x, axis, [(i, i ^ size) for i in range(count)])


def decayed(decay, rows, steps):
    return jnp.exp(-decay * (rows * steps).astype(F32))


def scan_four(final_f, final_b, decay, rows, axis, mine):
    jump = jnp.exp(-decay * float(rows))
    got = exchange(jnp.where(mine % 2 == 1, final_b, final_f), axis, 1)
    pair_f = final_f + jump * got
    pair_b = final_b + jump * got
    sent = jnp.where(mine == 1, pair_f, pair_b)
    across = lax.ppermute(sent, axis, [(1, 3), (2, 0)])
    diagonal = lax.ppermute(sent, axis, [(1, 2), (2, 1)])
    zero = jnp.zeros_like(final_f)
    incoming_f = jnp.where(
        mine == 3, got + jump * across, jnp.where(mine == 2, diagonal, jnp.where(mine == 1, got, zero))
    )
    incoming_b = jnp.where(
        mine == 0, got + jump * across, jnp.where(mine == 1, diagonal, jnp.where(mine == 2, got, zero))
    )
    return (incoming_f, incoming_b)


def scan_states(final_f, final_b, decay, rows, axis):
    count = lax.axis_size(axis)
    mine = lax.axis_index(axis)
    if count == 4:
        return scan_four(final_f, final_b, decay, rows, axis, mine)
    block_f, block_b = (final_f, final_b)
    incoming_f = jnp.zeros_like(final_f)
    incoming_b = jnp.zeros_like(final_b)
    levels = count.bit_length() - 1
    for level in range(levels):
        size = 1 << level
        upper = (mine // size) % 2 == 1
        pos = mine % size
        if level == levels - 1:
            sent = jnp.where(upper, block_b, block_f)
            half = sent.shape[1] // 2
            got = jnp.concatenate(
                [exchange(sent[:, :half], axis, size), exchange(sent[:, half:], axis, size)], 1
            )
            got_f, got_b = (got, got)
        else:
            got_f = exchange(block_f, axis, size)
            got_b = exchange(block_b, axis, size)
        incoming_f = incoming_f + jnp.where(upper, decayed(decay, rows, pos) * got_f, 0.0)
        incoming_b = incoming_b + jnp.where(upper, 0.0, decayed(decay, rows, size - 1 - pos) * got_b)
        if level < levels - 1:
            jump = jnp.exp(-decay * float(rows * size))
            block_f = jnp.where(upper, block_f + jump * got_f, got_f + jump * block_f)
            block_b = jnp.where(upper, got_b + jump * block_b, block_b + jump * got_b)
    return (incoming_f, incoming_b)


def butterfly_sum(x, steps):
    shape = x.shape
    flat = x.reshape(-1)
    pieces = 1 << len(steps)
    unit = pieces * 128
    padded = -(-flat.shape[0] // unit) * unit
    flat = jnp.pad(flat, (0, padded - flat.shape[0])).reshape(-1, 128)
    sides = []
    for axis, size in steps:
        upper = (lax.axis_index(axis) // size) % 2 == 1
        sides.append(upper)
        half = flat.shape[0] // 2
        low, high = (flat[:half], flat[half:])
        keep = jnp.where(upper, high, low)
        send = jnp.where(upper, low, high)
        flat = keep + exchange(send, axis, size)
    for (axis, size), upper in reversed(list(zip(steps, sides))):
        got = exchange(flat, axis, size)
        flat = jnp.where(upper, jnp.concatenate([got, flat]), jnp.concatenate([flat, got]))
    return flat.reshape(-1)[: x.size].reshape(shape)


def sum_steps():
    steps = []
    dp_count = lax.axis_size("dp")
    seq_count = lax.axis_size("seq")
    if dp_count & (dp_count - 1) or seq_count & (seq_count - 1):
        return None
    dp_bits = [1 << b for b in range(dp_count.bit_length() - 1)]
    seq_bits = [1 << b for b in range(seq_count.bit_length() - 1)]
    steps = [("dp", size) for size in dp_bits[:1]]
    steps += [("seq", size) for size in seq_bits]
    steps += [("dp", size) for size in dp_bits[1:]]
    return steps


def per_device(queries, keys, values, cotangent, taps, residue, skip, decay):
    rows = queries.shape[1]
    width = queries.shape[2]
    count = taps.shape[1]
    poles = decay.shape[0]
    q, k, v, c = queries[0], keys[0], values[0], cotangent[0]
    lead = jnp.stack([q[rows - RIM :], k[rows - RIM :], v[rows - RIM :]], 0)
    rim = passed_along(lead, "seq", 1)
    a = jnp.exp(-decay)
    f_bare, b_bare, bare_feats = run_states(q, k, v, c, jnp.zeros_like(lead), taps, a)
    with jax.named_scope("rim_share_of_states"):
        first = jnp.stack([q[:RIM], k[:RIM], v[:RIM]], 0).astype(F32)

        def head_feats(before):
            padded = jnp.concatenate([before, first], 1)
            return sum(taps[:, lag, None, :] * padded[:, RIM - lag : 2 * RIM - lag] for lag in range(count))

        with_rim = head_feats(rim.astype(F32))
        without = head_feats(jnp.zeros_like(first))
        d_product = with_rim[1] * with_rim[2] - without[1] * without[2]
        d_adjoint = c[:RIM].astype(F32) * (with_rim[0] - without[0])
        lags = jnp.arange(RIM, dtype=F32)
        f_local = f_bare + jnp.sum(
            jnp.exp(-decay[None] * (rows - 1 - lags)[:, None, None]) * d_product[:, None, :], 0
        )
        b_local = b_bare + jnp.sum(jnp.exp(-decay[None] * lags[:, None, None]) * d_adjoint[:, None, :], 0)
    with jax.named_scope("modal_state_scan"):
        s_in, g_in = scan_states(f_local, b_local, decay, rows, "seq")
    mixed, gq, gk, gv, tails, heads, grads = run_main(
        q, k, v, c, rim, taps, a, residue, skip.reshape(1, width), s_in, g_in, bare_feats
    )
    after = passed_along(heads, "seq", -1)
    ext = jnp.concatenate(
        [jnp.zeros((3, TAIL, width), F32), after[:, : count - 1], jnp.zeros((3, 1, width), F32)], 1
    )
    corr = sum(taps[:, lag, None, :] * ext[:, lag : lag + TAIL] for lag in range(count))
    fixed = (tails + corr).astype(jnp.bfloat16)
    streams = [
        lax.dynamic_update_slice(g, fixed[idx], (rows - TAIL, 0)) for idx, g in enumerate((gq, gk, gv))
    ]
    steps = sum_steps()
    if steps is None:
        totals = lax.psum(grads, ("seq", "dp"))
    else:
        with jax.named_scope("filter_grad_sum"):
            totals = butterfly_sum(grads, steps)
    grad_taps = totals[: 3 * count].reshape(3, count, width)
    grad_residue = totals[3 * count : 3 * count + poles]
    grad_skip = totals[3 * count + poles]
    return (
        mixed[None],
        streams[0][None],
        streams[1][None],
        streams[2][None],
        grad_taps,
        grad_residue,
        grad_skip,
    )


def solution(mesh):
    return jax.shard_map(
        per_device,
        mesh=mesh,
        in_specs=(
            P("dp", "seq", None),
            P("dp", "seq", None),
            P("dp", "seq", None),
            P("dp", "seq", None),
            P(),
            P(),
            P(),
            P(),
        ),
        out_specs=(
            P("dp", "seq", None),
            P("dp", "seq", None),
            P("dp", "seq", None),
            P("dp", "seq", None),
            P(),
            P(),
            P(),
        ),
        check_vma=False,
    )
```

```python
import functools

import jax
import jax.numpy as jnp
from jax import lax
from jax.experimental import pallas as pl
from jax.experimental.pallas import tpu as pltpu
from jax.sharding import PartitionSpec as P

LANES = 512
RIM = 8
TAIL = 16
BR = 16
F32 = jnp.float32


def passed_along(x, axis, by):
    count = lax.axis_size(axis)
    pairs = [(i, i + by) for i in range(count) if 0 <= i + by < count]
    return lax.ppermute(x, axis, pairs)


CHUNK = 256


def sublanes(lanes):
    return lax.broadcasted_iota(jnp.int32, (8, lanes), 0)


def feature_stream(pad_ref, taps_ref, s, out_ref, tiles=None):
    rows = out_ref.shape[1] if tiles is None else 8 * tiles
    count = taps_ref.shape[1]
    for c0 in range(0, out_ref.shape[2], CHUNK):
        cols = slice(c0, c0 + CHUNK)
        sub = sublanes(CHUNK)
        taps = [taps_ref[s, lag : lag + 1, cols] for lag in range(count)]
        prev = [pltpu.roll(pad_ref[s, 0:8, cols], lag, 0) for lag in range(1, count)]
        for i in range(rows // 8):
            cur = pad_ref[s, 8 * (i + 1) : 8 * (i + 2), cols]
            total = taps[0] * cur
            rolled = []
            for lag in range(1, count):
                turned = pltpu.roll(cur, lag, 0)
                total = total + taps[lag] * jnp.where(sub < lag, prev[lag - 1], turned)
                rolled.append(turned)
            prev = rolled
            out_ref[s, 8 * i : 8 * (i + 1), cols] = total


def fill_rows(x_refs, pad_ref, lo):
    for s, x_ref in enumerate(x_refs):
        pad_ref[s, RIM + lo : RIM + lo + BR, :] = x_ref[lo : lo + BR, :].astype(F32)


def states_kernel(
    q_ref, k_ref, v_ref, c_ref, rim_ref, taps_ref, a_ref, f_ref, b_ref, feat_ref, pad_ref, p_ref, z_ref
):
    rows = q_ref.shape[0]
    for s in range(3):
        pad_ref[s, 0:RIM, :] = rim_ref[s].astype(F32)
    for lo in range(0, rows, BR):
        fill_rows((q_ref, k_ref, v_ref), pad_ref, lo)
    for s in range(3):
        feature_stream(pad_ref, taps_ref, s, feat_ref)
    for lo in range(0, rows, BR):
        p_ref[lo : lo + BR, :] = feat_ref[1, lo : lo + BR, :] * feat_ref[2, lo : lo + BR, :]
        z_ref[lo : lo + BR, :] = c_ref[lo : lo + BR, :].astype(F32) * feat_ref[0, lo : lo + BR, :]
    a = a_ref[...]

    def step(i, carry):
        h, g = carry
        h = a * h + p_ref[pl.ds(i, 1), :]
        g = a * g + z_ref[pl.ds(rows - 1 - i, 1), :]
        return (h, g)

    zero = jnp.zeros_like(a)
    h, g = lax.fori_loop(0, rows, step, (zero, zero), unroll=8)
    f_ref[...] = h
    b_ref[...] = g


def fold(x):
    return x[0:8] + x[8:16]


def main_kernel(
    q_ref, k_ref, v_ref, c_ref, rim_ref, taps_ref, a_ref, r_ref, skip_ref, s_ref, g_ref, bare_ref,
    mixed_ref, gq_ref, gk_ref, gv_ref, tail_ref, head_ref, grads_ref,
    pad_ref, p_ref, z_ref, y_ref, u_ref, adj_ref, feat_ref,
):
    rows = q_ref.shape[0]
    count = taps_ref.shape[1]
    poles = a_ref.shape[0]
    lanes = q_ref.shape[1]
    for s in range(3):
        pad_ref[s, 0:RIM, :] = rim_ref[s].astype(F32)
    skip_sum = jnp.zeros((8, lanes), F32)
    for lo in range(0, rows, BR):
        fill_rows((q_ref, k_ref, v_ref), pad_ref, lo)
    for s in range(3):
        for lo in range(0, rows, BR):
            feat_ref[s, lo : lo + BR, :] = bare_ref[s, lo : lo + BR, :]
        feature_stream(pad_ref, taps_ref, s, feat_ref, tiles=1)
    for lo in range(0, rows, BR):
        fq = feat_ref[0, lo : lo + BR, :]
        fk = feat_ref[1, lo : lo + BR, :]
        fv = feat_ref[2, lo : lo + BR, :]
        p = fk * fv
        z = c_ref[lo : lo + BR, :].astype(F32) * fq
        p_ref[lo : lo + BR, :] = p
        z_ref[lo : lo + BR, :] = z
        skip_sum = skip_sum + fold(z * p)
    a = a_ref[...]
    r = r_ref[...]

    def step(i, carry):
        h, g, acc = carry
        h = a * h + p_ref[pl.ds(i, 1), :]
        acc = acc + z_ref[pl.ds(i, 1), :] * h
        y_ref[pl.ds(i, 1), :] = jnp.sum(r * h, axis=0, keepdims=True)
        back = rows - 1 - i
        g = a * g + z_ref[pl.ds(back, 1), :]
        u_ref[pl.ds(back, 1), :] = jnp.sum(r * g, axis=0, keepdims=True)
        return (h, g, acc)

    h, g, acc = lax.fori_loop(
        0, rows, step, (s_ref[...], g_ref[...], jnp.zeros_like(a)), unroll=16
    )
    skip = skip_ref[...]
    for lo in range(0, rows, BR):
        fq = feat_ref[0, lo : lo + BR, :]
        conv = y_ref[lo : lo + BR, :] + skip * p_ref[lo : lo + BR, :]
        mixed_ref[lo : lo + BR, :] = (fq * conv).astype(mixed_ref.dtype)
        adj_u = u_ref[lo : lo + BR, :] + skip * z_ref[lo : lo + BR, :]
        adj_ref[0, lo : lo + BR, :] = c_ref[lo : lo + BR, :].astype(F32) * conv
        adj_ref[1, lo : lo + BR, :] = adj_u * feat_ref[2, lo : lo + BR, :]
        adj_ref[2, lo : lo + BR, :] = adj_u * feat_ref[1, lo : lo + BR, :]
    zeros_rim = jnp.zeros((RIM, lanes), F32)
    outs = (gq_ref, gk_ref, gv_ref)
    for s in range(3):
        adj_ref[s, rows : rows + RIM, :] = zeros_rim
        head_ref[s] = adj_ref[s, 0:RIM, :]
    for s in range(3):
        for c0 in range(0, lanes, CHUNK):
            cols = slice(c0, c0 + CHUNK)
            sub = sublanes(CHUNK)
            taps = [taps_ref[s, lag : lag + 1, cols] for lag in range(count)]
            sums = [jnp.zeros((8, CHUNK), F32) for _ in range(count)]
            prev = [pltpu.roll(adj_ref[s, 0:8, cols], 8 - lag, 0) for lag in range(1, count)]
            done = []
            for i in range(rows // 8):
                cur = adj_ref[s, 8 * i : 8 * (i + 1), cols]
                after = adj_ref[s, 8 * (i + 1) : 8 * (i + 2), cols]
                x = pad_ref[s, RIM + 8 * i : RIM + 8 * (i + 1), cols]
                total = taps[0] * cur
                sums[0] = sums[0] + cur * x
                rolled = []
                for lag in range(1, count):
                    turned = pltpu.roll(after, 8 - lag, 0)
                    window = jnp.where(sub < 8 - lag, prev[lag - 1], turned)
                    total = total + taps[lag] * window
                    sums[lag] = sums[lag] + window * x
                    rolled.append(turned)
                prev = rolled
                done.append(total)
                if len(done) == 2:
                    both = jnp.concatenate(done, 0)
                    lo = 8 * (i - 1)
                    outs[s][lo : lo + BR, cols] = both.astype(outs[s].dtype)
                    if lo + BR == rows:
                        tail_ref[s, :, cols] = both[BR - TAIL :]
                    done = []
            for lag in range(count):
                value = jnp.sum(sums[lag], axis=0, keepdims=True)
                if lag > 0:
                    edge = adj_ref[s, 0:lag, cols] * pad_ref[s, RIM - lag : RIM, cols]
                    value = value + jnp.sum(edge, axis=0, keepdims=True)
                row = s * count + lag
                grads_ref[row : row + 1, cols] = value
    base = 3 * count
    grads_ref[base : base + poles, :] = acc
    grads_ref[base + poles : base + poles + 1, :] = jnp.sum(skip_sum, axis=0, keepdims=True)


def tile(shape, lanes):
    nd = len(shape)
    return pl.BlockSpec(tuple(shape[:-1]) + (lanes,), lambda i: (0,) * (nd - 1) + (i,))


def run_states(q, k, v, c, rim, taps, a):
    rows, width = q.shape
    poles = a.shape[0]
    lanes = min(LANES, width)
    ins = (q, k, v, c, rim, taps, a)
    return pl.pallas_call(
        states_kernel,
        grid=(width // lanes,),
        in_specs=[tile(x.shape, lanes) for x in ins],
        out_specs=[tile((poles, width), lanes), tile((poles, width), lanes), tile((3, rows, width), lanes)],
        out_shape=[jax.ShapeDtypeStruct((poles, width), F32)] * 2 + [jax.ShapeDtypeStruct((3, rows, width), F32)],
        scratch_shapes=[
            pltpu.VMEM((3, rows + RIM, lanes), F32),
            pltpu.VMEM((rows, lanes), F32),
            pltpu.VMEM((rows, lanes), F32),
        ],
    )(*ins)


def run_main(q, k, v, c, rim, taps, a, r, skip, s_in, g_in, bare):
    rows, width = q.shape
    poles = a.shape[0]
    count = taps.shape[1]
    lanes = min(LANES, width)
    ins = (q, k, v, c, rim, taps, a, r, skip, s_in, g_in, bare)
    out_shapes = [
        jax.ShapeDtypeStruct((rows, width), jnp.bfloat16),
        jax.ShapeDtypeStruct((rows, width), jnp.bfloat16),
        jax.ShapeDtypeStruct((rows, width), jnp.bfloat16),
        jax.ShapeDtypeStruct((rows, width), jnp.bfloat16),
        jax.ShapeDtypeStruct((3, TAIL, width), F32),
        jax.ShapeDtypeStruct((3, RIM, width), F32),
        jax.ShapeDtypeStruct((3 * count + poles + 1, width), F32),
    ]
    return pl.pallas_call(
        main_kernel,
        grid=(width // lanes,),
        in_specs=[tile(x.shape, lanes) for x in ins],
        out_specs=[tile(o.shape, lanes) for o in out_shapes],
        out_shape=out_shapes,
        scratch_shapes=[
            pltpu.VMEM((3, rows + RIM, lanes), F32),
            pltpu.VMEM((rows, lanes), F32),
            pltpu.VMEM((rows, lanes), F32),
            pltpu.VMEM((rows, lanes), F32),
            pltpu.VMEM((rows, lanes), F32),
            pltpu.VMEM((3, rows + RIM, lanes), F32),
            pltpu.VMEM((3, rows, lanes), F32),
        ],
    )(*ins)


def exchange(x, axis, size):
    count = lax.axis_size(axis)
    return lax.ppermute(x, axis, [(i, i ^ size) for i in range(count)])


def decayed(decay, rows, steps):
    return jnp.exp(-decay * (rows * steps).astype(F32))


def scan_four(final_f, final_b, decay, rows, axis, mine):
    jump = jnp.exp(-decay * float(rows))
    got = exchange(jnp.where(mine % 2 == 1, final_b, final_f), axis, 1)
    pair_f = final_f + jump * got
    pair_b = final_b + jump * got
    sent = jnp.where(mine == 1, pair_f, pair_b)
    across = lax.ppermute(sent, axis, [(1, 3), (2, 0)])
    diagonal = lax.ppermute(sent, axis, [(1, 2), (2, 1)])
    zero = jnp.zeros_like(final_f)
    incoming_f = jnp.where(
        mine == 3, got + jump * across, jnp.where(mine == 2, diagonal, jnp.where(mine == 1, got, zero))
    )
    incoming_b = jnp.where(
        mine == 0, got + jump * across, jnp.where(mine == 1, diagonal, jnp.where(mine == 2, got, zero))
    )
    return (incoming_f, incoming_b)


def scan_states(final_f, final_b, decay, rows, axis):
    count = lax.axis_size(axis)
    mine = lax.axis_index(axis)
    if count == 4:
        return scan_four(final_f, final_b, decay, rows, axis, mine)
    block_f, block_b = (final_f, final_b)
    incoming_f = jnp.zeros_like(final_f)
    incoming_b = jnp.zeros_like(final_b)
    levels = count.bit_length() - 1
    for level in range(levels):
        size = 1 << level
        upper = (mine // size) % 2 == 1
        pos = mine % size
        if level == levels - 1:
            sent = jnp.where(upper, block_b, block_f)
            half = sent.shape[1] // 2
            got = jnp.concatenate(
                [exchange(sent[:, :half], axis, size), exchange(sent[:, half:], axis, size)], 1
            )
            got_f, got_b = (got, got)
        else:
            got_f = exchange(block_f, axis, size)
            got_b = exchange(block_b, axis, size)
        incoming_f = incoming_f + jnp.where(upper, decayed(decay, rows, pos) * got_f, 0.0)
        incoming_b = incoming_b + jnp.where(upper, 0.0, decayed(decay, rows, size - 1 - pos) * got_b)
        if level < levels - 1:
            jump = jnp.exp(-decay * float(rows * size))
            block_f = jnp.where(upper, block_f + jump * got_f, got_f + jump * block_f)
            block_b = jnp.where(upper, got_b + jump * block_b, block_b + jump * got_b)
    return (incoming_f, incoming_b)


def butterfly_sum(x, steps):
    shape = x.shape
    flat = x.reshape(-1)
    pieces = 1 << len(steps)
    unit = pieces * 128
    padded = -(-flat.shape[0] // unit) * unit
    flat = jnp.pad(flat, (0, padded - flat.shape[0])).reshape(-1, 128)
    sides = []
    for axis, size in steps:
        upper = (lax.axis_index(axis) // size) % 2 == 1
        sides.append(upper)
        half = flat.shape[0] // 2
        low, high = (flat[:half], flat[half:])
        keep = jnp.where(upper, high, low)
        send = jnp.where(upper, low, high)
        flat = keep + exchange(send, axis, size)
    for (axis, size), upper in reversed(list(zip(steps, sides))):
        got = exchange(flat, axis, size)
        flat = jnp.where(upper, jnp.concatenate([got, flat]), jnp.concatenate([flat, got]))
    return flat.reshape(-1)[: x.size].reshape(shape)


def sum_steps():
    steps = []
    dp_count = lax.axis_size("dp")
    seq_count = lax.axis_size("seq")
    if dp_count & (dp_count - 1) or seq_count & (seq_count - 1):
        return None
    dp_bits = [1 << b for b in range(dp_count.bit_length() - 1)]
    seq_bits = [1 << b for b in range(seq_count.bit_length() - 1)]
    steps = [("dp", size) for size in dp_bits[:1]]
    steps += [("seq", size) for size in seq_bits]
    steps += [("dp", size) for size in dp_bits[1:]]
    return steps


def per_device(queries, keys, values, cotangent, taps, residue, skip, decay):
    rows = queries.shape[1]
    width = queries.shape[2]
    count = taps.shape[1]
    poles = decay.shape[0]
    q, k, v, c = queries[0], keys[0], values[0], cotangent[0]
    lead = jnp.stack([q[rows - RIM :], k[rows - RIM :], v[rows - RIM :]], 0)
    rim = passed_along(lead, "seq", 1)
    a = jnp.exp(-decay)
    f_bare, b_bare, bare_feats = run_states(q, k, v, c, jnp.zeros_like(lead), taps, a)
    with jax.named_scope("rim_share_of_states"):
        first = jnp.stack([q[:RIM], k[:RIM], v[:RIM]], 0).astype(F32)

        def head_feats(before):
            padded = jnp.concatenate([before, first], 1)
            return sum(taps[:, lag, None, :] * padded[:, RIM - lag : 2 * RIM - lag] for lag in range(count))

        with_rim = head_feats(rim.astype(F32))
        without = head_feats(jnp.zeros_like(first))
        d_product = with_rim[1] * with_rim[2] - without[1] * without[2]
        d_adjoint = c[:RIM].astype(F32) * (with_rim[0] - without[0])
        lags = jnp.arange(RIM, dtype=F32)
        f_local = f_bare + jnp.sum(
            jnp.exp(-decay[None] * (rows - 1 - lags)[:, None, None]) * d_product[:, None, :], 0
        )
        b_local = b_bare + jnp.sum(jnp.exp(-decay[None] * lags[:, None, None]) * d_adjoint[:, None, :], 0)
    with jax.named_scope("modal_state_scan"):
        s_in, g_in = scan_states(f_local, b_local, decay, rows, "seq")
    mixed, gq, gk, gv, tails, heads, grads = run_main(
        q, k, v, c, rim, taps, a, residue, skip.reshape(1, width), s_in, g_in, bare_feats
    )
    after = passed_along(heads, "seq", -1)
    ext = jnp.concatenate(
        [jnp.zeros((3, TAIL, width), F32), after[:, : count - 1], jnp.zeros((3, 1, width), F32)], 1
    )
    corr = sum(taps[:, lag, None, :] * ext[:, lag : lag + TAIL] for lag in range(count))
    fixed = (tails + corr).astype(jnp.bfloat16)
    streams = [
        lax.dynamic_update_slice(g, fixed[idx], (rows - TAIL, 0)) for idx, g in enumerate((gq, gk, gv))
    ]
    steps = sum_steps()
    if steps is None:
        totals = lax.psum(grads, ("seq", "dp"))
    else:
        with jax.named_scope("filter_grad_sum"):
            totals = butterfly_sum(grads, steps)
    grad_taps = totals[: 3 * count].reshape(3, count, width)
    grad_residue = totals[3 * count : 3 * count + poles]
    grad_skip = totals[3 * count + poles]
    return (
        mixed[None],
        streams[0][None],
        streams[1][None],
        streams[2][None],
        grad_taps,
        grad_residue,
        grad_skip,
    )


def solution(mesh):
    return jax.shard_map(
        per_device,
        mesh=mesh,
        in_specs=(
            P("dp", "seq", None),
            P("dp", "seq", None),
            P("dp", "seq", None),
            P("dp", "seq", None),
            P(),
            P(),
            P(),
            P(),
        ),
        out_specs=(
            P("dp", "seq", None),
            P("dp", "seq", None),
            P("dp", "seq", None),
            P("dp", "seq", None),
            P(),
            P(),
            P(),
        ),
        check_vma=False,
    )
```
